512 devices in a mesh: seq: 64 (over z, y), tensor: 8 (over x, core).
Axes of the slice: x: 4, y: 4, z: 16, core: 2. Of those that a mesh axis runs over, the one named last changes fastest.
Arguments:
- queries: bfloat16 [9216, 4096], P('seq', 'tensor'), may hold values from -44 to 44
- keys_values: bfloat16 [9216, 2, 4096], P('seq', None, 'tensor'), may hold values from -16 to 16
- segment_ids: int32 [9216], P('seq'), may hold values from 0 to 8, never falling along the last dimension, each value on 1 to 2161 neighbouring positions
- out_weight: bfloat16 [4096, 7168], P('tensor', 'seq'), may hold values from -0.09375 to 0.09375
Outputs:
- hidden_states: bfloat16 [9216, 7168], P('seq', 'tensor')
- kv_cache: bfloat16 [2, 32, 9216, 128], P(None, 'tensor', 'seq')
The draws below stay inside these ranges and needn't reach their ends.
Inputs may be any that keep to these rules, and one draw needn't show every extreme that they name: `segment_ids`: never falling along the tokens; each of the 9 prompts holds 1 to 2161 consecutive tokens, and one holds exactly 2161.
All inputs are finite; a program needn't handle non-finite values.
Results may differ from the reference program's by a relative error of at most 0.015.
Values may be sent and summed in bfloat16 or wider, within the bound.
No kernel may reach another device: no remote copies, remote signals or barrier semaphores. Data moves between devices by JAX's collectives and lax.ppermute only.
A program may use at most 64 MiB of HBM per device.

```python
import math
import jax
import jax.numpy as jnp
import numpy as np
from jax import lax

D = 7168
HD = 128
TOK_DEV = 144
SPAN = 16
HEADS = 32
TOKENS = 9216
MOST = 2161
SEGS = 9
N_SEQ = 64


def shared_draw(key):
    base_key = jax.random.fold_in(key, 11)
    key_list = jax.random.split(base_key, 4)
    shape = (TOKENS, HEADS * HD)
    key_rows = jnp.clip(jax.random.normal(key_list[0], shape, jnp.float32), -4.0, 4.0)
    drawn_queries = jnp.clip(jax.random.normal(key_list[1], shape, jnp.float32), -4.0, 4.0)
    value_scale = jnp.exp(jax.random.uniform(key_list[3], (TOKENS, 1), jnp.float32, math.log(0.4), math.log(4.0)))
    value_rows = jnp.clip(jax.random.normal(key_list[2], shape, jnp.float32), -4.0, 4.0) * value_scale
    query_rows = drawn_queries
    return (query_rows, key_rows, value_rows)


def draw_queries(key, part):
    query_rows, key_rows, value_rows = shared_draw(key)
    return query_rows.astype(jnp.bfloat16)


def draw_keys_values(key, part):
    query_rows, key_rows, value_rows = shared_draw(key)
    return jnp.stack([key_rows, value_rows], axis=1).astype(jnp.bfloat16)


def shard_levels(rng, dims, cuts, least, top_value):
    loudness = 1.0
    for dim, parts in cuts:
        heights = jax.random.uniform(jax.random.fold_in(jax.random.fold_in(rng, 6), dim), (parts,), jnp.float32, least / len(cuts), top_value / len(cuts))
        loudness = loudness * jnp.repeat(jnp.exp(heights), dims[dim] // parts).reshape((-1,) + (1,) * (len(dims) - 1 - dim))
    return loudness


def profile(count, total, limit, slope):
    portions = [(1 << 20) // math.isqrt(rank ** slope) + 1 for rank in range(2, count + 1)]
    rest, counts = total - limit - (count - 1), [1] * (count - 1)
    while rest > 0:
        candidates = [i for i in range(count - 1) if counts[i] < limit]
        mass, budget = sum([portions[i] for i in candidates]), rest
        for i in candidates:
            addition = min(limit - counts[i], max(1, budget * portions[i] // mass), rest)
            counts[i] = counts[i] + addition
            rest = rest - addition
    return np.array([limit] + counts)


def uneven(key, number_of, total, most, skew):
    if number_of == 2:
        one = jax.random.randint(key, (), max(1, total - most), min(most, total - 1) + 1)
        return jnp.stack([one, total - one])
    sizes = jnp.asarray(profile(number_of, total, most, skew), jnp.int32)
    pairs = (number_of - 1) // 2
    source_of, receiver = sizes[1:1 + 2 * pairs:2], sizes[2:2 + 2 * pairs:2]
    slack = jnp.minimum(source_of - 1, most - receiver)
    passed = jax.random.randint(jax.random.fold_in(key, 1), (pairs,), 0, 1 << 20) % (slack + 1)
    sizes = sizes.at[1:1 + 2 * pairs:2].set(source_of - passed).at[2:2 + 2 * pairs:2].set(receiver + passed)
    return sizes[jax.random.permutation(jax.random.fold_in(key, 2), number_of)]


def scatter_about(rng, extent, deviation, most, cuts=(), kind=jnp.bfloat16):
    drawn = deviation * jax.random.normal(rng, extent, jnp.float32)
    if cuts:
        drawn = drawn * shard_levels(rng, extent, cuts, -0.22, 0.18)
    return jnp.clip(drawn, -most, most).astype(kind)


def setup_inputs(seed: int = 0) -> dict:
    splits = jax.random.split(jax.random.key(seed), 5)
    return {
        "queries": draw_queries(jax.random.fold_in(splits[4], 71), 0),
        "keys_values": draw_keys_values(jax.random.fold_in(splits[4], 71), 0),
        "segment_ids": jnp.searchsorted(jnp.cumsum(uneven(splits[2], SEGS, TOKENS, MOST, 2)), jnp.arange(TOKENS), side="right").astype(jnp.int32),
        "out_weight": scatter_about(splits[3], (HEADS * HD, D), (HEADS * HD) ** -0.5, 0.09375, ((0, 8), (1, 64))),
    }


def reference(queries, keys_values, segment_ids, out_weight):
    token_count = queries.shape[0]
    feature_width = HEADS * HD
    front_pad = (SPAN - 1) * TOK_DEV
    padded_kv = jnp.pad(keys_values, ((front_pad, 0), (0, 0), (0, 0)))
    padded_seg = jnp.pad(segment_ids, (front_pad, 0), constant_values=-1)
    score_scale = 1.0 / math.sqrt(HD)

    def one_block(number):
        first_row = (number * TOK_DEV).astype(jnp.int32)
        query_rows = lax.dynamic_slice_in_dim(queries, first_row, TOK_DEV, 0).astype(jnp.float32)
        query_rows = query_rows.reshape(TOK_DEV, HEADS, HD)
        query_seg = lax.dynamic_slice_in_dim(segment_ids, first_row, TOK_DEV, 0)
        window = lax.dynamic_slice_in_dim(padded_kv, first_row, SPAN * TOK_DEV, 0).astype(jnp.float32)
        key_seg = lax.dynamic_slice_in_dim(padded_seg, first_row, SPAN * TOK_DEV, 0)
        key_rows = window[:, 0].reshape(SPAN * TOK_DEV, HEADS, HD)
        value_rows = window[:, 1].reshape(SPAN * TOK_DEV, HEADS, HD)
        query_pos = first_row + jnp.arange(TOK_DEV, dtype=jnp.int32)
        key_pos = first_row - front_pad + jnp.arange(SPAN * TOK_DEV, dtype=jnp.int32)
        allowed = (key_seg[None, :] == query_seg[:, None]) & (key_pos[None, :] <= query_pos[:, None])
        scores = jnp.einsum('qhd,khd->hqk', query_rows, key_rows) * score_scale
        masked = jnp.where(allowed[None], scores, -1e+30)
        row_top = lax.optimization_barrier(jnp.max(masked, axis=2, keepdims=True))
        probs = jnp.where(allowed[None], jnp.exp(masked - row_top), 0.0)
        row_total = lax.optimization_barrier(jnp.sum(probs, axis=2))
        weights = lax.optimization_barrier(probs.astype(jnp.bfloat16)).astype(jnp.float32)
        mixed = jnp.einsum('hqk,khd->hqd', weights, value_rows) / row_total[..., None]
        return mixed.transpose(1, 0, 2).reshape(TOK_DEV, feature_width).astype(jnp.bfloat16)
    attended = lax.map(one_block, jnp.arange(N_SEQ, dtype=jnp.int32)).reshape(token_count, feature_width)
    hidden_states = jnp.dot(attended, out_weight, preferred_element_type=jnp.float32).astype(jnp.bfloat16)
    kv_cache = keys_values.reshape(token_count, 2, HEADS, HD).transpose(1, 2, 0, 3)
    return (hidden_states, kv_cache)
```

```python
import math

import jax
import jax.numpy as jnp
from jax import lax
from jax.sharding import Mesh
from jax.sharding import PartitionSpec as P

HD = 128
NY = 4


def local(queries, keys_values, segment_ids, out_weight):
    rows = queries.shape[0]
    heads = queries.shape[1] // HD
    nz = lax.axis_size("z")
    z = lax.axis_index("z")
    level = NY * rows
    span = min(4, nz - 1)
    score_scale = 1.0 / math.sqrt(HD)

    packed = jnp.concatenate(
        [queries.reshape(rows, 1, heads, HD), keys_values.reshape(rows, 2, heads, HD)], axis=1
    ).reshape(rows, 3, NY, heads // NY, HD)
    packed = lax.all_to_all(packed, "y", 2, 0, tiled=True)
    hq = heads // NY
    query_rows = packed[:, 0, 0]
    pair = packed[:, 1:, 0]

    all_seg = lax.all_gather(segment_ids, ("z", "y"), tiled=True)
    offsets = jnp.arange(level, dtype=jnp.int32)
    query_pos = z * level + offsets
    query_seg = lax.dynamic_slice_in_dim(all_seg, z * level, level)

    def attend(carried, block, distance):
        run_max, row_total, accumulated = carried
        source = z - distance
        key_pos = source * level + offsets
        key_seg = lax.dynamic_slice_in_dim(all_seg, jnp.maximum(source, 0) * level, level)
        key_rows = block[:, 0]
        value_rows = block[:, 1]
        scores = (
            jnp.einsum("qhd,khd->hqk", query_rows, key_rows, preferred_element_type=jnp.float32)
            * score_scale
        )
        allowed = (
            (key_seg[None, :] == query_seg[:, None])
            & (key_pos[None, :] <= query_pos[:, None])
            & (source >= 0)
        )
        masked = jnp.where(allowed[None], scores, -1e30)
        new_max = jnp.maximum(run_max, jnp.max(masked, axis=2))
        probs = jnp.where(allowed[None], jnp.exp(masked - new_max[..., None]), 0.0)
        factor = jnp.exp(run_max - new_max)
        row_total = row_total * factor + jnp.sum(probs, axis=2)
        accumulated = accumulated * factor[..., None] + jnp.einsum(
            "hqk,khd->hqd",
            probs.astype(jnp.bfloat16),
            value_rows,
            preferred_element_type=jnp.float32,
        )
        return (new_max, row_total, accumulated)

    carried = (
        jnp.full((hq, level), -1e30, jnp.float32),
        jnp.zeros((hq, level), jnp.float32),
        jnp.zeros((hq, level, HD), jnp.float32),
    )
    carried = attend(carried, pair, 0)
    block = pair
    for distance in range(1, span + 1):
        block = lax.ppermute(block, "z", [(i, i + 1) for i in range(nz - 1)])
        carried = attend(carried, block, distance)
    run_max, row_total, accumulated = carried
    attended = (accumulated / row_total[..., None]).astype(jnp.bfloat16)
    attended = attended.transpose(1, 0, 2).reshape(level, hq * HD)

    level_attended = lax.all_gather(attended, "y", axis=1, tiled=True)
    weight_cols = lax.all_gather(out_weight, "z", axis=1, tiled=True)
    partial_value = jnp.dot(level_attended, weight_cols, preferred_element_type=jnp.float32)
    summed = lax.psum_scatter(
        partial_value.astype(jnp.bfloat16), "tensor", scatter_dimension=1, tiled=True
    )
    chunk = out_weight.shape[1]
    halves = summed.shape[1] // chunk
    summed = summed.reshape(NY, rows, halves, chunk)
    summed = lax.all_to_all(summed, "y", 0, 0, tiled=True)
    hidden_states = summed.transpose(1, 2, 0, 3).reshape(rows, halves * NY * chunk)

    head_major = keys_values.reshape(rows, 2, heads, HD).transpose(1, 2, 0, 3)
    return (hidden_states, head_major)


def solution(mesh):
    seq, tensor = mesh.shape["seq"], mesh.shape["tensor"]
    assert seq % NY == 0
    grid = Mesh(mesh.devices.reshape(seq // NY, NY, tensor), ("z", "y", "tensor"))
    s = ("z", "y")
    return jax.shard_map(
        local,
        mesh=grid,
        in_specs=(P(s, "tensor"), P(s, None, "tensor"), P(s), P("tensor", s)),
        out_specs=(P(s, "tensor"), P(None, "tensor", s, None)),
        check_vma=False,
    )
```

```python
import math

import jax
import jax.numpy as jnp
from jax import lax
from jax.sharding import Mesh
from jax.sharding import PartitionSpec as P

HD = 128
NY = 4


def local(queries, keys_values, segment_ids, out_weight):
    rows = queries.shape[0]
    heads = queries.shape[1] // HD
    nz = lax.axis_size("z")
    z = lax.axis_index("z")
    level = NY * rows
    span = min(4, nz - 1)
    score_scale = 1.0 / math.sqrt(HD)

    hq = heads // NY
    packed = jnp.concatenate(
        [queries.reshape(rows, 1, heads, HD), keys_values.reshape(rows, 2, heads, HD)], axis=1
    ).reshape(rows, 3, NY, hq, HD)
    seg_row = jnp.zeros((3 * hq * HD,), jnp.bfloat16).at[:rows].set(segment_ids.astype(jnp.bfloat16))
    seg_row = jnp.broadcast_to(seg_row.reshape(1, 3, 1, hq, HD), (1, 3, NY, hq, HD))
    packed = jnp.concatenate([packed, seg_row], axis=0)
    packed = lax.all_to_all(packed, "y", 2, 0, tiled=True).reshape(NY, rows + 1, 3, hq, HD)
    query_rows = packed[:, :rows, 0].reshape(level, hq, HD)
    pair = packed[:, :rows, 1:].reshape(level, 2, hq, HD)
    query_seg = packed[:, rows].reshape(NY, 3 * hq * HD)[:, :rows].reshape(level)

    extra = -(-level // (2 * hq * HD))
    seg_rows = jnp.zeros((extra * 2 * hq * HD,), jnp.bfloat16).at[:level].set(query_seg)
    pair = jnp.concatenate([pair, seg_rows.reshape(extra, 2, hq, HD)], axis=0)
    query_seg = query_seg.astype(jnp.int32)
    offsets = jnp.arange(level, dtype=jnp.int32)
    query_pos = z * level + offsets

    def attend(carried, block, distance):
        run_max, row_total, accumulated = carried
        source = z - distance
        key_pos = source * level + offsets
        key_seg = block[level:].reshape(-1)[:level].astype(jnp.int32)
        key_rows = block[:level, 0]
        value_rows = block[:level, 1]
        scores = (
            jnp.einsum("qhd,khd->hqk", query_rows, key_rows, preferred_element_type=jnp.float32)
            * score_scale
        )
        allowed = (
            (key_seg[None, :] == query_seg[:, None])
            & (key_pos[None, :] <= query_pos[:, None])
            & (source >= 0)
        )
        masked = jnp.where(allowed[None], scores, -1e30)
        new_max = jnp.maximum(run_max, jnp.max(masked, axis=2))
        probs = jnp.where(allowed[None], jnp.exp(masked - new_max[..., None]), 0.0)
        factor = jnp.exp(run_max - new_max)
        row_total = row_total * factor + jnp.sum(probs, axis=2)
        accumulated = accumulated * factor[..., None] + jnp.einsum(
            "hqk,khd->hqd",
            probs.astype(jnp.bfloat16),
            value_rows,
            preferred_element_type=jnp.float32,
        )
        return (new_max, row_total, accumulated)

    carried = (
        jnp.full((hq, level), -1e30, jnp.float32),
        jnp.zeros((hq, level), jnp.float32),
        jnp.zeros((hq, level, HD), jnp.float32),
    )
    carried = attend(carried, pair, 0)
    block = pair
    for distance in range(1, span + 1):
        block = lax.ppermute(block, "z", [(i, i + 1) for i in range(nz - 1)])
        carried = attend(carried, block, distance)
    run_max, row_total, accumulated = carried
    attended = (accumulated / row_total[..., None]).astype(jnp.bfloat16)
    attended = attended.transpose(1, 0, 2).reshape(level, hq * HD)

    level_attended = lax.all_gather(attended, "y", axis=1, tiled=True)
    weight_cols = lax.all_gather(out_weight, "z", axis=1, tiled=True)
    partial_value = jnp.dot(level_attended, weight_cols, preferred_element_type=jnp.float32)
    summed = lax.psum_scatter(
        partial_value.astype(jnp.bfloat16), "tensor", scatter_dimension=1, tiled=True
    )
    chunk = out_weight.shape[1]
    halves = summed.shape[1] // chunk
    summed = summed.reshape(NY, rows, halves, chunk)
    summed = lax.all_to_all(summed, "y", 0, 0, tiled=True)
    hidden_states = summed.transpose(1, 2, 0, 3).reshape(rows, halves * NY * chunk)

    head_major = keys_values.reshape(rows, 2, heads, HD).transpose(1, 2, 0, 3)
    return (hidden_states, head_major)


def solution(mesh):
    seq, tensor = mesh.shape["seq"], mesh.shape["tensor"]
    assert seq % NY == 0
    grid = Mesh(mesh.devices.reshape(seq // NY, NY, tensor), ("z", "y", "tensor"))
    s = ("z", "y")
    return jax.shard_map(
        local,
        mesh=grid,
        in_specs=(P(s, "tensor"), P(s, None, "tensor"), P(s), P("tensor", s)),
        out_specs=(P(s, "tensor"), P(None, "tensor", s, None)),
        check_vma=False,
    )
```

```python
import math

import jax
import jax.numpy as jnp
from jax import lax
from jax.sharding import Mesh
from jax.sharding import PartitionSpec as P

HD = 128
NY = 4


def local(queries, keys_values, segment_ids, out_weight):
    rows = queries.shape[0]
    heads = queries.shape[1] // HD
    nz = lax.axis_size("z")
    z = lax.axis_index("z")
    level = NY * rows
    span = min(4, nz - 1)
    score_scale = 1.0 / math.sqrt(HD)

    hq = heads // NY
    packed = jnp.concatenate(
        [queries.reshape(rows, 1, heads, HD), keys_values.reshape(rows, 2, heads, HD)], axis=1
    ).reshape(rows, 3, NY, hq, HD)
    seg_row = jnp.zeros((3 * hq * HD,), jnp.bfloat16).at[:rows].set(segment_ids.astype(jnp.bfloat16))
    seg_row = jnp.broadcast_to(seg_row.reshape(1, 3, 1, hq, HD), (1, 3, NY, hq, HD))
    packed = jnp.concatenate([packed, seg_row], axis=0)
    packed = lax.all_to_all(packed, "y", 2, 0, tiled=True).reshape(NY, rows + 1, 3, hq, HD)
    query_rows = packed[:, :rows, 0].reshape(level, hq, HD)
    pair = packed[:, :rows, 1:].reshape(level, 2, hq, HD)
    query_seg = packed[:, rows].reshape(NY, 3 * hq * HD)[:, :rows].reshape(level)

    extra = -(-level // (2 * hq * HD))
    seg_rows = jnp.zeros((extra * 2 * hq * HD,), jnp.bfloat16).at[:level].set(query_seg)
    pair = jnp.concatenate([pair, seg_rows.reshape(extra, 2, hq, HD)], axis=0)
    query_seg = query_seg.astype(jnp.int32)
    offsets = jnp.arange(level, dtype=jnp.int32)
    query_pos = z * level + offsets

    def attend(carried, block, distance):
        run_max, row_total, accumulated = carried
        source = z - distance
        key_pos = source * level + offsets
        key_seg = block[level:].reshape(-1)[:level].astype(jnp.int32)
        key_rows = block[:level, 0]
        value_rows = block[:level, 1]
        scores = (
            jnp.einsum("qhd,khd->hqk", query_rows, key_rows, preferred_element_type=jnp.float32)
            * score_scale
        )
        allowed = (
            (key_seg[None, :] == query_seg[:, None])
            & (key_pos[None, :] <= query_pos[:, None])
            & (source >= 0)
        )
        masked = jnp.where(allowed[None], scores, -1e30)
        new_max = jnp.maximum(run_max, jnp.max(masked, axis=2))
        probs = jnp.where(allowed[None], jnp.exp(masked - new_max[..., None]), 0.0)
        factor = jnp.exp(run_max - new_max)
        row_total = row_total * factor + jnp.sum(probs, axis=2)
        accumulated = accumulated * factor[..., None] + jnp.einsum(
            "hqk,khd->hqd",
            probs.astype(jnp.bfloat16),
            value_rows,
            preferred_element_type=jnp.float32,
        )
        return (new_max, row_total, accumulated)

    carried = (
        jnp.full((hq, level), -1e30, jnp.float32),
        jnp.zeros((hq, level), jnp.float32),
        jnp.zeros((hq, level, HD), jnp.float32),
    )
    carried = attend(carried, pair, 0)
    block = pair
    for distance in range(1, span + 1):
        block = lax.ppermute(block, "z", [(i, i + 1) for i in range(nz - 1)])
        carried = attend(carried, block, distance)
    run_max, row_total, accumulated = carried
    attended = (accumulated / row_total[..., None]).astype(jnp.bfloat16)
    attended = attended.transpose(1, 0, 2).reshape(level, hq * HD)

    c = lax.axis_index("c")
    swap = [(0, 1), (1, 0)]
    own_attended = lax.all_gather(attended, "y", axis=1, tiled=True)
    other_attended = lax.ppermute(own_attended, "c", swap)
    weight_cols = lax.all_gather(out_weight, "z", axis=1, tiled=True)
    chunk = out_weight.shape[1]
    weight_cols = weight_cols.reshape(weight_cols.shape[0], nz // 2, 2, chunk)
    own_weight = lax.dynamic_index_in_dim(weight_cols, c, axis=2, keepdims=False)
    other_weight = lax.ppermute(
        lax.dynamic_index_in_dim(weight_cols, 1 - c, axis=2, keepdims=False), "c", swap
    )
    own_weight = own_weight.reshape(own_weight.shape[0], -1)
    other_weight = other_weight.reshape(other_weight.shape[0], -1)
    partial_value = jnp.dot(own_attended, own_weight, preferred_element_type=jnp.float32)
    partial_value = partial_value + jnp.dot(
        other_attended, other_weight, preferred_element_type=jnp.float32
    )
    summed = lax.psum_scatter(
        partial_value.astype(jnp.bfloat16), "x", scatter_dimension=1, tiled=True
    )
    summed = summed.reshape(NY, rows, 2, chunk).transpose(0, 2, 1, 3).reshape(2 * NY, rows, chunk)
    summed = lax.all_to_all(summed, ("y", "c"), 0, 0, tiled=True)
    hidden_states = summed.reshape(NY, 2, rows, chunk).transpose(2, 1, 0, 3).reshape(rows, 2 * NY * chunk)

    head_major = keys_values.reshape(rows, 2, heads, HD).transpose(1, 2, 0, 3)
    return (hidden_states, head_major)


def solution(mesh):
    seq, tensor = mesh.shape["seq"], mesh.shape["tensor"]
    assert seq % NY == 0 and tensor % 2 == 0
    grid = Mesh(
        mesh.devices.reshape(seq // NY, NY, tensor // 2, 2), ("z", "y", "x", "c")
    )
    s, t = ("z", "y"), ("x", "c")
    return jax.shard_map(
        local,
        mesh=grid,
        in_specs=(P(s, t), P(s, None, t), P(s), P(t, s)),
        out_specs=(P(s, t), P(None, t, s, None)),
        check_vma=False,
    )
```

```python
import math

import jax
import jax.numpy as jnp
from jax import lax
from jax.sharding import Mesh
from jax.sharding import PartitionSpec as P

HD = 128
NY = 4


def local(queries, keys_values, segment_ids, out_weight):
    rows = queries.shape[0]
    heads = queries.shape[1] // HD
    nz = lax.axis_size("z")
    z = lax.axis_index("z")
    level = NY * rows
    span = min(4, nz - 1)
    score_scale = 1.0 / math.sqrt(HD)

    hq = heads // NY
    packed = jnp.concatenate(
        [queries.reshape(rows, 1, heads, HD), keys_values.reshape(rows, 2, heads, HD)], axis=1
    ).reshape(rows, 3, NY, hq, HD)
    seg_row = jnp.zeros((3 * hq * HD,), jnp.bfloat16).at[:rows].set(segment_ids.astype(jnp.bfloat16))
    seg_row = jnp.broadcast_to(seg_row.reshape(1, 3, 1, hq, HD), (1, 3, NY, hq, HD))
    packed = jnp.concatenate([packed, seg_row], axis=0)
    packed = lax.all_to_all(packed, "y", 2, 0, tiled=True).reshape(NY, rows + 1, 3, hq, HD)
    query_rows = packed[:, :rows, 0].reshape(level, hq, HD)
    pair = packed[:, :rows, 1:].reshape(level, 2, hq, HD)
    query_seg = packed[:, rows].reshape(NY, 3 * hq * HD)[:, :rows].reshape(level)

    extra = -(-level // (2 * hq * HD))
    seg_rows = jnp.zeros((extra * 2 * hq * HD,), jnp.bfloat16).at[:level].set(query_seg)
    pair = jnp.concatenate([pair, seg_rows.reshape(extra, 2, hq, HD)], axis=0)
    query_seg = query_seg.astype(jnp.int32)
    offsets = jnp.arange(level, dtype=jnp.int32)
    query_pos = z * level + offsets

    def attend(carried, block, distance):
        run_max, row_total, accumulated = carried
        source = z - distance
        key_pos = source * level + offsets
        key_seg = block[level:].reshape(-1)[:level].astype(jnp.int32)
        key_rows = block[:level, 0]
        value_rows = block[:level, 1]
        scores = (
            jnp.einsum("qhd,khd->hqk", query_rows, key_rows, preferred_element_type=jnp.float32)
            * score_scale
        )
        allowed = (
            (key_seg[None, :] == query_seg[:, None])
            & (key_pos[None, :] <= query_pos[:, None])
            & (source >= 0)
        )
        masked = jnp.where(allowed[None], scores, -1e30)
        new_max = jnp.maximum(run_max, jnp.max(masked, axis=2))
        probs = jnp.where(allowed[None], jnp.exp(masked - new_max[..., None]), 0.0)
        factor = jnp.exp(run_max - new_max)
        row_total = row_total * factor + jnp.sum(probs, axis=2)
        accumulated = accumulated * factor[..., None] + jnp.einsum(
            "hqk,khd->hqd",
            probs.astype(jnp.bfloat16),
            value_rows,
            preferred_element_type=jnp.float32,
        )
        return (new_max, row_total, accumulated)

    carried = (
        jnp.full((hq, level), -1e30, jnp.float32),
        jnp.zeros((hq, level), jnp.float32),
        jnp.zeros((hq, level, HD), jnp.float32),
    )
    carried = attend(carried, pair, 0)
    block = pair
    for distance in range(1, span + 1):
        block = lax.ppermute(block, "z", [(i, i + 1) for i in range(nz - 1)])
        carried = attend(carried, block, distance)
    run_max, row_total, accumulated = carried
    attended = (accumulated / row_total[..., None]).astype(jnp.bfloat16)
    attended = attended.transpose(1, 0, 2).reshape(level, hq * HD)

    c = lax.axis_index("c")
    swap = [(0, 1), (1, 0)]
    own_attended = lax.all_gather(attended, "y", axis=1, tiled=True)
    weight_cols = lax.all_gather(out_weight, "z", axis=1, tiled=True)
    weight_cols, own_attended = lax.optimization_barrier((weight_cols, own_attended))
    other_attended = lax.ppermute(own_attended, "c", swap)
    chunk = out_weight.shape[1]
    weight_cols = weight_cols.reshape(weight_cols.shape[0], nz // 2, 2, chunk)
    own_weight = lax.dynamic_index_in_dim(weight_cols, c, axis=2, keepdims=False)
    other_weight = lax.ppermute(
        lax.dynamic_index_in_dim(weight_cols, 1 - c, axis=2, keepdims=False), "c", swap
    )
    own_weight = own_weight.reshape(own_weight.shape[0], -1)
    other_weight = other_weight.reshape(other_weight.shape[0], -1)
    partial_value = jnp.dot(own_attended, own_weight, preferred_element_type=jnp.float32)
    partial_value = partial_value + jnp.dot(
        other_attended, other_weight, preferred_element_type=jnp.float32
    )
    summed = lax.psum_scatter(
        partial_value.astype(jnp.bfloat16), "x", scatter_dimension=1, tiled=True
    )
    summed = summed.reshape(NY, rows, 2, chunk).transpose(0, 2, 1, 3).reshape(2 * NY, rows, chunk)
    summed = lax.all_to_all(summed, ("y", "c"), 0, 0, tiled=True)
    hidden_states = summed.reshape(NY, 2, rows, chunk).transpose(2, 1, 0, 3).reshape(rows, 2 * NY * chunk)

    head_major = keys_values.reshape(rows, 2, heads, HD).transpose(1, 2, 0, 3)
    return (hidden_states, head_major)


def solution(mesh):
    seq, tensor = mesh.shape["seq"], mesh.shape["tensor"]
    assert seq % NY == 0 and tensor % 2 == 0
    grid = Mesh(
        mesh.devices.reshape(seq // NY, NY, tensor // 2, 2), ("z", "y", "x", "c")
    )
    s, t = ("z", "y"), ("x", "c")
    return jax.shard_map(
        local,
        mesh=grid,
        in_specs=(P(s, t), P(s, None, t), P(s), P(t, s)),
        out_specs=(P(s, t), P(None, t, s, None)),
        check_vma=False,
    )
```

```python
import math

import jax
import jax.numpy as jnp
from jax import lax
from jax.sharding import Mesh
from jax.sharding import PartitionSpec as P

HD = 128
NY = 4


def local(queries, keys_values, segment_ids, out_weight):
    rows = queries.shape[0]
    heads = queries.shape[1] // HD
    nz = lax.axis_size("z")
    z = lax.axis_index("z")
    level = NY * rows
    span = min(4, nz - 1)
    score_scale = 1.0 / math.sqrt(HD)

    hq = heads // NY
    packed = jnp.concatenate(
        [queries.reshape(rows, 1, heads, HD), keys_values.reshape(rows, 2, heads, HD)], axis=1
    ).reshape(rows, 3, NY, hq, HD)
    seg_row = jnp.zeros((3 * hq * HD,), jnp.bfloat16).at[:rows].set(segment_ids.astype(jnp.bfloat16))
    seg_row = jnp.broadcast_to(seg_row.reshape(1, 3, 1, hq, HD), (1, 3, NY, hq, HD))
    packed = jnp.concatenate([packed, seg_row], axis=0)
    packed = lax.all_to_all(packed, "y", 2, 0, tiled=True).reshape(NY, rows + 1, 3, hq, HD)
    query_rows = packed[:, :rows, 0].reshape(level, hq, HD)
    pair = packed[:, :rows, 1:].reshape(level, 2, hq, HD)
    query_seg = packed[:, rows].reshape(NY, 3 * hq * HD)[:, :rows].reshape(level)

    extra = -(-level // (2 * hq * HD))
    seg_rows = jnp.zeros((extra * 2 * hq * HD,), jnp.bfloat16).at[:level].set(query_seg)
    pair = jnp.concatenate([pair, seg_rows.reshape(extra, 2, hq, HD)], axis=0)
    query_seg = query_seg.astype(jnp.int32)
    offsets = jnp.arange(level, dtype=jnp.int32)
    query_pos = z * level + offsets

    def attend(carried, block, distance):
        run_max, row_total, accumulated = carried
        source = z - distance
        key_pos = source * level + offsets
        key_seg = block[level:].reshape(-1)[:level].astype(jnp.int32)
        key_rows = block[:level, 0]
        value_rows = block[:level, 1]
        scores = (
            jnp.einsum("qhd,khd->hqk", query_rows, key_rows, preferred_element_type=jnp.float32)
            * score_scale
        )
        allowed = (
            (key_seg[None, :] == query_seg[:, None])
            & (key_pos[None, :] <= query_pos[:, None])
            & (source >= 0)
        )
        masked = jnp.where(allowed[None], scores, -1e30)
        new_max = jnp.maximum(run_max, jnp.max(masked, axis=2))
        probs = jnp.where(allowed[None], jnp.exp(masked - new_max[..., None]), 0.0)
        factor = jnp.exp(run_max - new_max)
        row_total = row_total * factor + jnp.sum(probs, axis=2)
        accumulated = accumulated * factor[..., None] + jnp.einsum(
            "hqk,khd->hqd",
            probs.astype(jnp.bfloat16),
            value_rows,
            preferred_element_type=jnp.float32,
        )
        return (new_max, row_total, accumulated)

    carried = (
        jnp.full((hq, level), -1e30, jnp.float32),
        jnp.zeros((hq, level), jnp.float32),
        jnp.zeros((hq, level, HD), jnp.float32),
    )
    carried = attend(carried, pair, 0)
    block = pair
    for distance in range(1, span + 1):
        block = lax.ppermute(block, "z", [(i, i + 1) for i in range(nz - 1)])
        carried = attend(carried, block, distance)
    run_max, row_total, accumulated = carried
    attended = (accumulated / row_total[..., None]).astype(jnp.bfloat16)
    attended = attended.transpose(1, 0, 2).reshape(level, hq * HD)

    c = lax.axis_index("c")
    swap = [(0, 1), (1, 0)]
    own_attended = lax.all_gather(attended, "y", axis=1, tiled=True)
    weight_cols = lax.all_gather(out_weight, "z", axis=1, tiled=True)
    weight_cols, own_attended = lax.optimization_barrier((weight_cols, own_attended))
    other_attended = lax.ppermute(own_attended, "c", swap)
    chunk = out_weight.shape[1]
    weight_cols = weight_cols.reshape(weight_cols.shape[0], nz // 2, 2, chunk)
    own_weight = lax.dynamic_index_in_dim(weight_cols, c, axis=2, keepdims=False)
    other_weight = lax.ppermute(
        lax.dynamic_index_in_dim(weight_cols, 1 - c, axis=2, keepdims=False), "c", swap
    )
    own_weight = own_weight.reshape(own_weight.shape[0], -1)
    other_weight = other_weight.reshape(other_weight.shape[0], -1)
    partial_value = jnp.dot(own_attended, own_weight, preferred_element_type=jnp.float32)
    partial_value = partial_value + jnp.dot(
        other_attended, other_weight, preferred_element_type=jnp.float32
    )
    nx = lax.axis_size("x")
    x = lax.axis_index("x")
    quarters = partial_value.astype(jnp.bfloat16).reshape(level, nx, -1)
    summed = lax.dynamic_index_in_dim(quarters, x, axis=1, keepdims=False).astype(jnp.float32)
    for shift in range(1, nx):
        part = lax.dynamic_index_in_dim(quarters, (x + shift) % nx, axis=1, keepdims=False)
        part = lax.ppermute(part, "x", [(i, (i + shift) % nx) for i in range(nx)])
        summed = summed + part.astype(jnp.float32)
    summed = summed.astype(jnp.bfloat16)
    summed = summed.reshape(NY, rows, 2, chunk).transpose(0, 2, 1, 3).reshape(2 * NY, rows, chunk)
    summed = lax.all_to_all(summed, ("y", "c"), 0, 0, tiled=True)
    hidden_states = summed.reshape(NY, 2, rows, chunk).transpose(2, 1, 0, 3).reshape(rows, 2 * NY * chunk)

    head_major = keys_values.reshape(rows, 2, heads, HD).transpose(1, 2, 0, 3)
    return (hidden_states, head_major)


def solution(mesh):
    seq, tensor = mesh.shape["seq"], mesh.shape["tensor"]
    assert seq % NY == 0 and tensor % 2 == 0
    grid = Mesh(
        mesh.devices.reshape(seq // NY, NY, tensor // 2, 2), ("z", "y", "x", "c")
    )
    s, t = ("z", "y"), ("x", "c")
    return jax.shard_map(
        local,
        mesh=grid,
        in_specs=(P(s, t), P(s, None, t), P(s), P(t, s)),
        out_specs=(P(s, t), P(None, t, s, None)),
        check_vma=False,
    )
```

```python
import math

import jax
import jax.numpy as jnp
from jax import lax
from jax.sharding import Mesh
from jax.sharding import PartitionSpec as P

HD = 128
NY = 4


def local(queries, keys_values, segment_ids, out_weight):
    rows = queries.shape[0]
    heads = queries.shape[1] // HD
    nz = lax.axis_size("z")
    z = lax.axis_index("z")
    level = NY * rows
    span = min(4, nz - 1)
    score_scale = 1.0 / math.sqrt(HD)

    hq = heads // NY
    packed = jnp.concatenate(
        [queries.reshape(rows, 1, heads, HD), keys_values.reshape(rows, 2, heads, HD)], axis=1
    ).reshape(rows, 3, NY, hq, HD)
    seg_row = jnp.zeros((3 * hq * HD,), jnp.bfloat16).at[:rows].set(segment_ids.astype(jnp.bfloat16))
    seg_row = jnp.broadcast_to(seg_row.reshape(1, 3, 1, hq, HD), (1, 3, NY, hq, HD))
    packed = jnp.concatenate([packed, seg_row], axis=0)
    packed = lax.all_to_all(packed, "y", 2, 0, tiled=True).reshape(NY, rows + 1, 3, hq, HD)
    query_rows = packed[:, :rows, 0].reshape(level, hq, HD)
    pair = packed[:, :rows, 1:].reshape(level, 2, hq, HD)
    query_seg = packed[:, rows].reshape(NY, 3 * hq * HD)[:, :rows].reshape(level)

    extra = -(-level // (2 * hq * HD))
    seg_rows = jnp.zeros((extra * 2 * hq * HD,), jnp.bfloat16).at[:level].set(query_seg)
    pair = jnp.concatenate([pair, seg_rows.reshape(extra, 2, hq, HD)], axis=0)
    query_seg = query_seg.astype(jnp.int32)
    offsets = jnp.arange(level, dtype=jnp.int32)

    def attend(carried, block, distance):
        run_max, row_total, accumulated = carried
        source = z - distance
        key_seg = block[level:].reshape(-1)[:level].astype(jnp.int32)
        key_rows = block[:level, 0]
        value_rows = block[:level, 1]
        scores = (
            jnp.einsum("qhd,khd->hqk", query_rows, key_rows, preferred_element_type=jnp.float32)
            * score_scale
        )
        allowed = key_seg[None, :] == query_seg[:, None]
        if distance == 0:
            allowed = allowed & (offsets[None, :] <= offsets[:, None])
        else:
            allowed = allowed & (source >= 0)
        masked = jnp.where(allowed[None], scores, -1e30)
        new_max = jnp.maximum(run_max, jnp.max(masked, axis=2))
        probs = jnp.where(allowed[None], jnp.exp(masked - new_max[..., None]), 0.0)
        factor = jnp.exp(run_max - new_max)
        row_total = row_total * factor + jnp.sum(probs, axis=2)
        accumulated = accumulated * factor[..., None] + jnp.einsum(
            "hqk,khd->hqd",
            probs.astype(jnp.bfloat16),
            value_rows,
            preferred_element_type=jnp.float32,
        )
        return (new_max, row_total, accumulated)

    carried = (
        jnp.full((hq, level), -1e30, jnp.float32),
        jnp.zeros((hq, level), jnp.float32),
        jnp.zeros((hq, level, HD), jnp.float32),
    )
    carried = attend(carried, pair, 0)
    block = pair
    for distance in range(1, span + 1):
        block = lax.ppermute(block, "z", [(i, i + 1) for i in range(nz - 1)])
        carried = attend(carried, block, distance)
    run_max, row_total, accumulated = carried
    attended = (accumulated / row_total[..., None]).astype(jnp.bfloat16)
    attended = attended.transpose(1, 0, 2).reshape(level, hq * HD)

    c = lax.axis_index("c")
    swap = [(0, 1), (1, 0)]
    own_attended = lax.all_gather(attended, "y", axis=1, tiled=True)
    weight_cols = lax.all_gather(out_weight, "z", axis=1, tiled=True)
    weight_cols, own_attended = lax.optimization_barrier((weight_cols, own_attended))
    other_attended = lax.ppermute(own_attended, "c", swap)
    chunk = out_weight.shape[1]
    weight_cols = weight_cols.reshape(weight_cols.shape[0], nz // 2, 2, chunk)
    own_weight = lax.dynamic_index_in_dim(weight_cols, c, axis=2, keepdims=False)
    other_weight = lax.ppermute(
        lax.dynamic_index_in_dim(weight_cols, 1 - c, axis=2, keepdims=False), "c", swap
    )
    own_weight = own_weight.reshape(own_weight.shape[0], -1)
    other_weight = other_weight.reshape(other_weight.shape[0], -1)
    partial_value = jnp.dot(own_attended, own_weight, preferred_element_type=jnp.float32)
    partial_value = partial_value + jnp.dot(
        other_attended, other_weight, preferred_element_type=jnp.float32
    )
    nx = lax.axis_size("x")
    x = lax.axis_index("x")
    quarters = partial_value.astype(jnp.bfloat16).reshape(level, nx, -1)
    summed = lax.dynamic_index_in_dim(quarters, x, axis=1, keepdims=False).astype(jnp.float32)
    for shift in range(1, nx):
        part = lax.dynamic_index_in_dim(quarters, (x + shift) % nx, axis=1, keepdims=False)
        part = lax.ppermute(part, "x", [(i, (i + shift) % nx) for i in range(nx)])
        summed = summed + part.astype(jnp.float32)
    summed = summed.astype(jnp.bfloat16)
    summed = summed.reshape(NY, rows, 2, chunk).transpose(0, 2, 1, 3).reshape(2 * NY, rows, chunk)
    summed = lax.all_to_all(summed, ("y", "c"), 0, 0, tiled=True)
    hidden_states = summed.reshape(NY, 2, rows, chunk).transpose(2, 1, 0, 3).reshape(rows, 2 * NY * chunk)

    head_major = keys_values.reshape(rows, 2, heads, HD).transpose(1, 2, 0, 3)
    return (hidden_states, head_major)


def solution(mesh):
    seq, tensor = mesh.shape["seq"], mesh.shape["tensor"]
    assert seq % NY == 0 and tensor % 2 == 0
    grid = Mesh(
        mesh.devices.reshape(seq // NY, NY, tensor // 2, 2), ("z", "y", "x", "c")
    )
    s, t = ("z", "y"), ("x", "c")
    return jax.shard_map(
        local,
        mesh=grid,
        in_specs=(P(s, t), P(s, None, t), P(s), P(t, s)),
        out_specs=(P(s, t), P(None, t, s, None)),
        check_vma=False,
    )
```

```python
import math

import jax
import jax.numpy as jnp
from jax import lax
from jax.sharding import Mesh
from jax.sharding import PartitionSpec as P

HD = 128
NY = 4


def by_source(pieces, me):
    n = len(pieces)
    stacked = jnp.stack(pieces)
    return jnp.take(stacked, (me - jnp.arange(n)) % n, axis=0)


def from_all_y(value, me, piece=None):
    pieces = [value if piece is None else piece(me)]
    for shift in range(1, NY):
        out = value if piece is None else piece((me + shift) % NY)
        pieces.append(lax.ppermute(out, "y", [(i, (i + shift) % NY) for i in range(NY)]))
    return by_source(pieces, me)


def local(queries, keys_values, segment_ids, out_weight):
    rows = queries.shape[0]
    heads = queries.shape[1] // HD
    nz = lax.axis_size("z")
    z = lax.axis_index("z")
    level = NY * rows
    span = min(4, nz - 1)
    score_scale = 1.0 / math.sqrt(HD)

    hq = heads // NY
    packed = jnp.concatenate(
        [queries.reshape(rows, 1, heads, HD), keys_values.reshape(rows, 2, heads, HD)], axis=1
    ).reshape(rows, 3, NY, hq, HD)
    seg_row = jnp.zeros((3 * hq * HD,), jnp.bfloat16).at[:rows].set(segment_ids.astype(jnp.bfloat16))
    seg_row = jnp.broadcast_to(seg_row.reshape(1, 3, 1, hq, HD), (1, 3, NY, hq, HD))
    packed = jnp.concatenate([packed, seg_row], axis=0)
    y = lax.axis_index("y")
    packed = from_all_y(
        packed, y, lambda dest: lax.dynamic_index_in_dim(packed, dest, axis=2, keepdims=False)
    )
    query_rows = packed[:, :rows, 0].reshape(level, hq, HD)
    pair = packed[:, :rows, 1:].reshape(level, 2, hq, HD)
    query_seg = packed[:, rows].reshape(NY, 3 * hq * HD)[:, :rows].reshape(level)

    extra = -(-level // (2 * hq * HD))
    seg_rows = jnp.zeros((extra * 2 * hq * HD,), jnp.bfloat16).at[:level].set(query_seg)
    pair = jnp.concatenate([pair, seg_rows.reshape(extra, 2, hq, HD)], axis=0)
    query_seg = query_seg.astype(jnp.int32)
    offsets = jnp.arange(level, dtype=jnp.int32)

    def attend(carried, block, distance):
        run_max, row_total, accumulated = carried
        source = z - distance
        key_seg = block[level:].reshape(-1)[:level].astype(jnp.int32)
        key_rows = block[:level, 0]
        value_rows = block[:level, 1]
        scores = (
            jnp.einsum("qhd,khd->hqk", query_rows, key_rows, preferred_element_type=jnp.float32)
            * score_scale
        )
        allowed = key_seg[None, :] == query_seg[:, None]
        if distance == 0:
            allowed = allowed & (offsets[None, :] <= offsets[:, None])
        else:
            allowed = allowed & (source >= 0)
        masked = jnp.where(allowed[None], scores, -1e30)
        new_max = jnp.maximum(run_max, jnp.max(masked, axis=2))
        probs = jnp.where(allowed[None], jnp.exp(masked - new_max[..., None]), 0.0)
        factor = jnp.exp(run_max - new_max)
        row_total = row_total * factor + jnp.sum(probs, axis=2)
        accumulated = accumulated * factor[..., None] + jnp.einsum(
            "hqk,khd->hqd",
            probs.astype(jnp.bfloat16),
            value_rows,
            preferred_element_type=jnp.float32,
        )
        return (new_max, row_total, accumulated)

    carried = (
        jnp.full((hq, level), -1e30, jnp.float32),
        jnp.zeros((hq, level), jnp.float32),
        jnp.zeros((hq, level, HD), jnp.float32),
    )
    carried = attend(carried, pair, 0)
    block = pair
    for distance in range(1, span + 1):
        block = lax.ppermute(block, "z", [(i, i + 1) for i in range(nz - 1)])
        carried = attend(carried, block, distance)
    run_max, row_total, accumulated = carried
    attended = (accumulated / row_total[..., None]).astype(jnp.bfloat16)
    attended = attended.transpose(1, 0, 2).reshape(level, hq * HD)

    c = lax.axis_index("c")
    swap = [(0, 1), (1, 0)]
    own_attended = from_all_y(attended, y).transpose(1, 0, 2).reshape(level, NY * hq * HD)
    weight_cols = lax.all_gather(out_weight, "z", axis=1, tiled=True)
    weight_cols, own_attended = lax.optimization_barrier((weight_cols, own_attended))
    other_attended = lax.ppermute(own_attended, "c", swap)
    chunk = out_weight.shape[1]
    weight_cols = weight_cols.reshape(weight_cols.shape[0], nz // 2, 2, chunk)
    own_weight = lax.dynamic_index_in_dim(weight_cols, c, axis=2, keepdims=False)
    other_weight = lax.ppermute(
        lax.dynamic_index_in_dim(weight_cols, 1 - c, axis=2, keepdims=False), "c", swap
    )
    own_weight = own_weight.reshape(own_weight.shape[0], -1)
    other_weight = other_weight.reshape(other_weight.shape[0], -1)
    partial_value = jnp.dot(own_attended, own_weight, preferred_element_type=jnp.float32)
    partial_value = partial_value + jnp.dot(
        other_attended, other_weight, preferred_element_type=jnp.float32
    )
    nx = lax.axis_size("x")
    x = lax.axis_index("x")
    quarters = partial_value.astype(jnp.bfloat16).reshape(level, nx, -1)
    summed = lax.dynamic_index_in_dim(quarters, x, axis=1, keepdims=False).astype(jnp.float32)
    for shift in range(1, nx):
        part = lax.dynamic_index_in_dim(quarters, (x + shift) % nx, axis=1, keepdims=False)
        part = lax.ppermute(part, "x", [(i, (i + shift) % nx) for i in range(nx)])
        summed = summed + part.astype(jnp.float32)
    summed = summed.astype(jnp.bfloat16)
    summed = summed.reshape(NY, rows, 2, chunk).transpose(0, 2, 1, 3).reshape(2 * NY, rows, chunk)
    summed = lax.all_to_all(summed, ("y", "c"), 0, 0, tiled=True)
    hidden_states = summed.reshape(NY, 2, rows, chunk).transpose(2, 1, 0, 3).reshape(rows, 2 * NY * chunk)

    head_major = keys_values.reshape(rows, 2, heads, HD).transpose(1, 2, 0, 3)
    return (hidden_states, head_major)


def solution(mesh):
    seq, tensor = mesh.shape["seq"], mesh.shape["tensor"]
    assert seq % NY == 0 and tensor % 2 == 0
    grid = Mesh(
        mesh.devices.reshape(seq // NY, NY, tensor // 2, 2), ("z", "y", "x", "c")
    )
    s, t = ("z", "y"), ("x", "c")
    return jax.shard_map(
        local,
        mesh=grid,
        in_specs=(P(s, t), P(s, None, t), P(s), P(t, s)),
        out_specs=(P(s, t), P(None, t, s, None)),
        check_vma=False,
    )
```

```python
import math

import jax
import jax.numpy as jnp
from jax import lax
from jax.sharding import Mesh
from jax.sharding import PartitionSpec as P

HD = 128
NY = 4


def local(queries, keys_values, segment_ids, out_weight):
    rows = queries.shape[0]
    heads = queries.shape[1] // HD
    nz = lax.axis_size("z")
    z = lax.axis_index("z")
    level = NY * rows
    span = min(4, nz - 1)
    score_scale = 1.0 / math.sqrt(HD)

    hq = heads // NY
    packed = jnp.concatenate(
        [queries.reshape(rows, 1, heads, HD), keys_values.reshape(rows, 2, heads, HD)], axis=1
    ).reshape(rows, 3, NY, hq, HD)
    seg_row = jnp.zeros((3 * hq * HD,), jnp.bfloat16).at[:rows].set(segment_ids.astype(jnp.bfloat16))
    seg_row = jnp.broadcast_to(seg_row.reshape(1, 3, 1, hq, HD), (1, 3, NY, hq, HD))
    packed = jnp.concatenate([packed, seg_row], axis=0)
    packed = lax.all_to_all(packed, "y", 2, 0, tiled=True).reshape(NY, rows + 1, 3, hq, HD)
    query_rows = packed[:, :rows, 0].reshape(level, hq, HD)
    pair = packed[:, :rows, 1:].reshape(level, 2, hq, HD)
    query_seg = packed[:, rows].reshape(NY, 3 * hq * HD)[:, :rows].reshape(level)

    extra = -(-level // (2 * hq * HD))
    seg_rows = jnp.zeros((extra * 2 * hq * HD,), jnp.bfloat16).at[:level].set(query_seg)
    pair = jnp.concatenate([pair, seg_rows.reshape(extra, 2, hq, HD)], axis=0)
    query_seg = query_seg.astype(jnp.int32)
    offsets = jnp.arange(level, dtype=jnp.int32)

    def attend(carried, block, distance):
        run_max, row_total, accumulated = carried
        source = z - distance
        key_seg = block[level:].reshape(-1)[:level].astype(jnp.int32)
        key_rows = block[:level, 0]
        value_rows = block[:level, 1]
        scores = (
            jnp.einsum("qhd,khd->hqk", query_rows, key_rows, preferred_element_type=jnp.float32)
            * score_scale
        )
        allowed = key_seg[None, :] == query_seg[:, None]
        if distance == 0:
            allowed = allowed & (offsets[None, :] <= offsets[:, None])
        else:
            allowed = allowed & (source >= 0)
        masked = jnp.where(allowed[None], scores, -1e30)
        new_max = jnp.maximum(run_max, jnp.max(masked, axis=2))
        probs = jnp.where(allowed[None], jnp.exp(masked - new_max[..., None]), 0.0)
        factor = jnp.exp(run_max - new_max)
        row_total = row_total * factor + jnp.sum(probs, axis=2)
        accumulated = accumulated * factor[..., None] + jnp.einsum(
            "hqk,khd->hqd",
            probs.astype(jnp.bfloat16),
            value_rows,
            preferred_element_type=jnp.float32,
        )
        return (new_max, row_total, accumulated)

    carried = (
        jnp.full((hq, level), -1e30, jnp.float32),
        jnp.zeros((hq, level), jnp.float32),
        jnp.zeros((hq, level, HD), jnp.float32),
    )
    relay = [(i, i + 1) for i in range(nz - 1)]
    carried = attend(carried, pair, 0)
    block = lax.ppermute(pair, "z", relay)
    for distance in range(2, span + 1):
        block, carried = lax.optimization_barrier((block, carried))
        arriving = lax.ppermute(block, "z", relay)
        carried = attend(carried, block, distance - 1)
        block = arriving
    carried = attend(carried, block, span)
    run_max, row_total, accumulated = carried
    attended = (accumulated / row_total[..., None]).astype(jnp.bfloat16)
    attended = attended.transpose(1, 0, 2).reshape(level, hq * HD)

    c = lax.axis_index("c")
    swap = [(0, 1), (1, 0)]
    own_attended = lax.all_gather(attended, "y", axis=1, tiled=True)
    weight_cols = lax.all_gather(out_weight, "z", axis=1, tiled=True)
    weight_cols, own_attended = lax.optimization_barrier((weight_cols, own_attended))
    other_attended = lax.ppermute(own_attended, "c", swap)
    chunk = out_weight.shape[1]
    weight_cols = weight_cols.reshape(weight_cols.shape[0], nz // 2, 2, chunk)
    own_weight = lax.dynamic_index_in_dim(weight_cols, c, axis=2, keepdims=False)
    other_weight = lax.ppermute(
        lax.dynamic_index_in_dim(weight_cols, 1 - c, axis=2, keepdims=False), "c", swap
    )
    own_weight = own_weight.reshape(own_weight.shape[0], -1)
    other_weight = other_weight.reshape(other_weight.shape[0], -1)
    partial_value = jnp.dot(own_attended, own_weight, preferred_element_type=jnp.float32)
    partial_value = partial_value + jnp.dot(
        other_attended, other_weight, preferred_element_type=jnp.float32
    )
    nx = lax.axis_size("x")
    x = lax.axis_index("x")
    quarters = partial_value.astype(jnp.bfloat16).reshape(level, nx, -1)
    summed = lax.dynamic_index_in_dim(quarters, x, axis=1, keepdims=False).astype(jnp.float32)
    for shift in range(1, nx):
        part = lax.dynamic_index_in_dim(quarters, (x + shift) % nx, axis=1, keepdims=False)
        part = lax.ppermute(part, "x", [(i, (i + shift) % nx) for i in range(nx)])
        summed = summed + part.astype(jnp.float32)
    summed = summed.astype(jnp.bfloat16)
    summed = summed.reshape(NY, rows, 2, chunk).transpose(0, 2, 1, 3).reshape(2 * NY, rows, chunk)
    summed = lax.all_to_all(summed, ("y", "c"), 0, 0, tiled=True)
    hidden_states = summed.reshape(NY, 2, rows, chunk).transpose(2, 1, 0, 3).reshape(rows, 2 * NY * chunk)

    head_major = keys_values.reshape(rows, 2, heads, HD).transpose(1, 2, 0, 3)
    return (hidden_states, head_major)


def solution(mesh):
    seq, tensor = mesh.shape["seq"], mesh.shape["tensor"]
    assert seq % NY == 0 and tensor % 2 == 0
    grid = Mesh(
        mesh.devices.reshape(seq // NY, NY, tensor // 2, 2), ("z", "y", "x", "c")
    )
    s, t = ("z", "y"), ("x", "c")
    return jax.shard_map(
        local,
        mesh=grid,
        in_specs=(P(s, t), P(s, None, t), P(s), P(t, s)),
        out_specs=(P(s, t), P(None, t, s, None)),
        check_vma=False,
    )
```

```python
import math

import jax
import jax.numpy as jnp
from jax import lax
from jax.sharding import Mesh
from jax.sharding import PartitionSpec as P

HD = 128
NY = 4


def local(queries, keys_values, segment_ids, out_weight):
    rows = queries.shape[0]
    heads = queries.shape[1] // HD
    nz = 2 * lax.axis_size("zh")
    z = lax.axis_index("zh") * 2 + lax.axis_index("zl")
    level = NY * rows
    span = min(4, nz - 1)
    score_scale = 1.0 / math.sqrt(HD)

    hq = heads // NY
    packed = jnp.concatenate(
        [queries.reshape(rows, 1, heads, HD), keys_values.reshape(rows, 2, heads, HD)], axis=1
    ).reshape(rows, 3, NY, hq, HD)
    seg_row = jnp.zeros((3 * hq * HD,), jnp.bfloat16).at[:rows].set(segment_ids.astype(jnp.bfloat16))
    seg_row = jnp.broadcast_to(seg_row.reshape(1, 3, 1, hq, HD), (1, 3, NY, hq, HD))
    packed = jnp.concatenate([packed, seg_row], axis=0)
    packed = lax.all_to_all(packed, "y", 2, 0, tiled=True).reshape(NY, rows + 1, 3, hq, HD)
    query_rows = packed[:, :rows, 0].reshape(level, hq, HD)
    pair = packed[:, :rows, 1:].reshape(level, 2, hq, HD)
    query_seg = packed[:, rows].reshape(NY, 3 * hq * HD)[:, :rows].reshape(level)

    extra = -(-level // (2 * hq * HD))
    seg_rows = jnp.zeros((extra * 2 * hq * HD,), jnp.bfloat16).at[:level].set(query_seg)
    pair = jnp.concatenate([pair, seg_rows.reshape(extra, 2, hq, HD)], axis=0)
    query_seg = query_seg.astype(jnp.int32)
    offsets = jnp.arange(level, dtype=jnp.int32)

    def attend(carried, block, distance):
        run_max, row_total, accumulated = carried
        source = z - distance
        key_seg = block[level:].reshape(-1)[:level].astype(jnp.int32)
        key_rows = block[:level, 0]
        value_rows = block[:level, 1]
        scores = (
            jnp.einsum("qhd,khd->hqk", query_rows, key_rows, preferred_element_type=jnp.float32)
            * score_scale
        )
        allowed = key_seg[None, :] == query_seg[:, None]
        if distance == 0:
            allowed = allowed & (offsets[None, :] <= offsets[:, None])
        else:
            allowed = allowed & (source >= 0)
        masked = jnp.where(allowed[None], scores, -1e30)
        new_max = jnp.maximum(run_max, jnp.max(masked, axis=2))
        probs = jnp.where(allowed[None], jnp.exp(masked - new_max[..., None]), 0.0)
        factor = jnp.exp(run_max - new_max)
        row_total = row_total * factor + jnp.sum(probs, axis=2)
        accumulated = accumulated * factor[..., None] + jnp.einsum(
            "hqk,khd->hqd",
            probs.astype(jnp.bfloat16),
            value_rows,
            preferred_element_type=jnp.float32,
        )
        return (new_max, row_total, accumulated)

    carried = (
        jnp.full((hq, level), -1e30, jnp.float32),
        jnp.zeros((hq, level), jnp.float32),
        jnp.zeros((hq, level, HD), jnp.float32),
    )
    relay = [(i, i + 1) for i in range(nz - 1)]
    carried = attend(carried, pair, 0)
    block = lax.ppermute(pair, ("zh", "zl"), relay)
    for distance in range(2, span + 1):
        block, carried = lax.optimization_barrier((block, carried))
        arriving = lax.ppermute(block, ("zh", "zl"), relay)
        carried = attend(carried, block, distance - 1)
        block = arriving
    carried = attend(carried, block, span)
    run_max, row_total, accumulated = carried
    attended = (accumulated / row_total[..., None]).astype(jnp.bfloat16)
    attended = attended.transpose(1, 0, 2).reshape(level, hq * HD)

    c = lax.axis_index("c")
    swap = [(0, 1), (1, 0)]
    own_attended = lax.all_gather(attended, "y", axis=1, tiled=True)
    other_attended = lax.ppermute(own_attended, "c", swap)
    weight_cols = lax.all_gather(out_weight, "zl", axis=1, tiled=True)
    weight_cols = lax.all_gather(weight_cols, "zh", axis=1, tiled=True)
    weight_cols, own_attended, other_attended = lax.optimization_barrier(
        (weight_cols, own_attended, other_attended)
    )
    chunk = out_weight.shape[1]
    weight_cols = weight_cols.reshape(weight_cols.shape[0], nz // 2, 2, chunk)
    own_weight = lax.dynamic_index_in_dim(weight_cols, c, axis=2, keepdims=False)
    other_weight = lax.ppermute(
        lax.dynamic_index_in_dim(weight_cols, 1 - c, axis=2, keepdims=False), "c", swap
    )
    own_weight = own_weight.reshape(own_weight.shape[0], -1)
    other_weight = other_weight.reshape(other_weight.shape[0], -1)
    partial_value = jnp.dot(own_attended, own_weight, preferred_element_type=jnp.float32)
    partial_value = partial_value + jnp.dot(
        other_attended, other_weight, preferred_element_type=jnp.float32
    )
    nx = lax.axis_size("x")
    x = lax.axis_index("x")
    quarters = partial_value.astype(jnp.bfloat16).reshape(level, nx, -1)
    summed = lax.dynamic_index_in_dim(quarters, x, axis=1, keepdims=False).astype(jnp.float32)
    for shift in range(1, nx):
        part = lax.dynamic_index_in_dim(quarters, (x + shift) % nx, axis=1, keepdims=False)
        part = lax.ppermute(part, "x", [(i, (i + shift) % nx) for i in range(nx)])
        summed = summed + part.astype(jnp.float32)
    summed = summed.astype(jnp.bfloat16)
    summed = summed.reshape(NY, rows, 2, chunk).transpose(0, 2, 1, 3).reshape(2 * NY, rows, chunk)
    summed = lax.all_to_all(summed, ("y", "c"), 0, 0, tiled=True)
    hidden_states = summed.reshape(NY, 2, rows, chunk).transpose(2, 1, 0, 3).reshape(rows, 2 * NY * chunk)

    head_major = keys_values.reshape(rows, 2, heads, HD).transpose(1, 2, 0, 3)
    return (hidden_states, head_major)


def solution(mesh):
    seq, tensor = mesh.shape["seq"], mesh.shape["tensor"]
    assert seq % NY == 0 and tensor % 2 == 0
    assert (seq // NY) % 2 == 0
    grid = Mesh(
        mesh.devices.reshape(seq // NY // 2, 2, NY, tensor // 2, 2), ("zh", "zl", "y", "x", "c")
    )
    s, t = ("zh", "zl", "y"), ("x", "c")
    return jax.shard_map(
        local,
        mesh=grid,
        in_specs=(P(s, t), P(s, None, t), P(s), P(t, s)),
        out_specs=(P(s, t), P(None, t, s, None)),
        check_vma=False,
    )
```

```python
import math

import jax
import jax.numpy as jnp
from jax import lax
from jax.sharding import Mesh
from jax.sharding import PartitionSpec as P

HD = 128
NY = 4


def local(queries, keys_values, segment_ids, out_weight):
    rows = queries.shape[0]
    heads = queries.shape[1] // HD
    nz = lax.axis_size("z")
    z = lax.axis_index("z")
    level = NY * rows
    span = min(4, nz - 1)
    score_scale = 1.0 / math.sqrt(HD)
    weight_cols = lax.all_gather(out_weight, "z", axis=1, tiled=True)

    hq = heads // NY
    packed = jnp.concatenate(
        [queries.reshape(rows, 1, heads, HD), keys_values.reshape(rows, 2, heads, HD)], axis=1
    ).reshape(rows, 3, NY, hq, HD)
    seg_row = jnp.zeros((3 * hq * HD,), jnp.bfloat16).at[:rows].set(segment_ids.astype(jnp.bfloat16))
    seg_row = jnp.broadcast_to(seg_row.reshape(1, 3, 1, hq, HD), (1, 3, NY, hq, HD))
    packed = jnp.concatenate([packed, seg_row], axis=0)
    packed = lax.all_to_all(packed, "y", 2, 0, tiled=True).reshape(NY, rows + 1, 3, hq, HD)
    query_rows = packed[:, :rows, 0].reshape(level, hq, HD)
    pair = packed[:, :rows, 1:].reshape(level, 2, hq, HD)
    query_seg = packed[:, rows].reshape(NY, 3 * hq * HD)[:, :rows].reshape(level)

    extra = -(-level // (2 * hq * HD))
    seg_rows = jnp.zeros((extra * 2 * hq * HD,), jnp.bfloat16).at[:level].set(query_seg)
    pair = jnp.concatenate([pair, seg_rows.reshape(extra, 2, hq, HD)], axis=0)
    query_seg = query_seg.astype(jnp.int32)
    offsets = jnp.arange(level, dtype=jnp.int32)

    def attend(carried, block, distance):
        run_max, row_total, accumulated = carried
        source = z - distance
        key_seg = block[level:].reshape(-1)[:level].astype(jnp.int32)
        key_rows = block[:level, 0]
        value_rows = block[:level, 1]
        scores = (
            jnp.einsum("qhd,khd->hqk", query_rows, key_rows, preferred_element_type=jnp.float32)
            * score_scale
        )
        allowed = key_seg[None, :] == query_seg[:, None]
        if distance == 0:
            allowed = allowed & (offsets[None, :] <= offsets[:, None])
        else:
            allowed = allowed & (source >= 0)
        masked = jnp.where(allowed[None], scores, -1e30)
        new_max = jnp.maximum(run_max, jnp.max(masked, axis=2))
        probs = jnp.where(allowed[None], jnp.exp(masked - new_max[..., None]), 0.0)
        factor = jnp.exp(run_max - new_max)
        row_total = row_total * factor + jnp.sum(probs, axis=2)
        accumulated = accumulated * factor[..., None] + jnp.einsum(
            "hqk,khd->hqd",
            probs.astype(jnp.bfloat16),
            value_rows,
            preferred_element_type=jnp.float32,
        )
        return (new_max, row_total, accumulated)

    carried = (
        jnp.full((hq, level), -1e30, jnp.float32),
        jnp.zeros((hq, level), jnp.float32),
        jnp.zeros((hq, level, HD), jnp.float32),
    )
    relay = [(i, i + 1) for i in range(nz - 1)]
    carried = attend(carried, pair, 0)
    block = lax.ppermute(pair, "z", relay)
    for distance in range(2, span + 1):
        block, carried = lax.optimization_barrier((block, carried))
        arriving = lax.ppermute(block, "z", relay)
        carried = attend(carried, block, distance - 1)
        block = arriving
    carried = attend(carried, block, span)
    run_max, row_total, accumulated = carried
    attended = (accumulated / row_total[..., None]).astype(jnp.bfloat16)
    attended = attended.transpose(1, 0, 2).reshape(level, hq * HD)

    c = lax.axis_index("c")
    swap = [(0, 1), (1, 0)]
    own_attended = lax.all_gather(attended, "y", axis=1, tiled=True)
    other_attended = lax.ppermute(own_attended, "c", swap)
    weight_cols, own_attended, other_attended = lax.optimization_barrier(
        (weight_cols, own_attended, other_attended)
    )
    chunk = out_weight.shape[1]
    weight_cols = weight_cols.reshape(weight_cols.shape[0], nz // 2, 2, chunk)
    own_weight = lax.dynamic_index_in_dim(weight_cols, c, axis=2, keepdims=False)
    other_weight = lax.ppermute(
        lax.dynamic_index_in_dim(weight_cols, 1 - c, axis=2, keepdims=False), "c", swap
    )
    own_weight = own_weight.reshape(own_weight.shape[0], -1)
    other_weight = other_weight.reshape(other_weight.shape[0], -1)
    partial_value = jnp.dot(own_attended, own_weight, preferred_element_type=jnp.float32)
    partial_value = partial_value + jnp.dot(
        other_attended, other_weight, preferred_element_type=jnp.float32
    )
    nx = lax.axis_size("x")
    x = lax.axis_index("x")
    quarters = partial_value.astype(jnp.bfloat16).reshape(level, nx, -1)
    summed = lax.dynamic_index_in_dim(quarters, x, axis=1, keepdims=False).astype(jnp.float32)
    for shift in range(1, nx):
        part = lax.dynamic_index_in_dim(quarters, (x + shift) % nx, axis=1, keepdims=False)
        part = lax.ppermute(part, "x", [(i, (i + shift) % nx) for i in range(nx)])
        summed = summed + part.astype(jnp.float32)
    summed = summed.astype(jnp.bfloat16)
    summed = summed.reshape(NY, rows, 2, chunk).transpose(0, 2, 1, 3).reshape(2 * NY, rows, chunk)
    summed = lax.all_to_all(summed, ("y", "c"), 0, 0, tiled=True)
    hidden_states = summed.reshape(NY, 2, rows, chunk).transpose(2, 1, 0, 3).reshape(rows, 2 * NY * chunk)

    head_major = keys_values.reshape(rows, 2, heads, HD).transpose(1, 2, 0, 3)
    return (hidden_states, head_major)


def solution(mesh):
    seq, tensor = mesh.shape["seq"], mesh.shape["tensor"]
    assert seq % NY == 0 and tensor % 2 == 0
    grid = Mesh(
        mesh.devices.reshape(seq // NY, NY, tensor // 2, 2), ("z", "y", "x", "c")
    )
    s, t = ("z", "y"), ("x", "c")
    return jax.shard_map(
        local,
        mesh=grid,
        in_specs=(P(s, t), P(s, None, t), P(s), P(t, s)),
        out_specs=(P(s, t), P(None, t, s, None)),
        check_vma=False,
    )
```

```python
import math

import jax
import jax.numpy as jnp
from jax import lax
from jax.sharding import Mesh
from jax.sharding import PartitionSpec as P

HD = 128
NY = 4


def local(queries, keys_values, segment_ids, out_weight):
    rows = queries.shape[0]
    heads = queries.shape[1] // HD
    nz = lax.axis_size("z")
    z = lax.axis_index("z")
    level = NY * rows
    span = min(4, nz - 1)
    score_scale = 1.0 / math.sqrt(HD)
    weight_cols = lax.all_gather(out_weight, "z", axis=1, tiled=True)

    hq = heads // NY
    packed = jnp.concatenate(
        [queries.reshape(rows, 1, heads, HD), keys_values.reshape(rows, 2, heads, HD)], axis=1
    ).reshape(rows, 3, NY, hq, HD)
    seg_row = jnp.zeros((3 * hq * HD,), jnp.bfloat16).at[:rows].set(segment_ids.astype(jnp.bfloat16))
    seg_row = jnp.broadcast_to(seg_row.reshape(1, 3, 1, hq, HD), (1, 3, NY, hq, HD))
    packed = jnp.concatenate([packed, seg_row], axis=0)
    packed = lax.all_to_all(packed, "y", 2, 0, tiled=True).reshape(NY, rows + 1, 3, hq, HD)
    query_rows = packed[:, :rows, 0].reshape(level, hq, HD)
    pair = packed[:, :rows, 1:].reshape(level, 2, hq, HD)
    query_seg = packed[:, rows].reshape(NY, 3 * hq * HD)[:, :rows].reshape(level)

    extra = -(-level // (2 * hq * HD))
    seg_rows = jnp.zeros((extra * 2 * hq * HD,), jnp.bfloat16).at[:level].set(query_seg)
    pair = jnp.concatenate([pair, seg_rows.reshape(extra, 2, hq, HD)], axis=0)
    query_seg = query_seg.astype(jnp.int32)
    offsets = jnp.arange(level, dtype=jnp.int32)

    def attend(carried, block, distance):
        run_max, row_total, accumulated = carried
        source = z - distance
        key_seg = block[level:].reshape(-1)[:level].astype(jnp.int32)
        key_rows = block[:level, 0]
        value_rows = block[:level, 1]
        scores = (
            jnp.einsum("qhd,khd->hqk", query_rows, key_rows, preferred_element_type=jnp.float32)
            * score_scale
        )
        allowed = key_seg[None, :] == query_seg[:, None]
        if distance == 0:
            allowed = allowed & (offsets[None, :] <= offsets[:, None])
        else:
            allowed = allowed & (source >= 0)
        masked = jnp.where(allowed[None], scores, -1e30)
        new_max = jnp.maximum(run_max, jnp.max(masked, axis=2))
        probs = jnp.where(allowed[None], jnp.exp(masked - new_max[..., None]), 0.0)
        factor = jnp.exp(run_max - new_max)
        row_total = row_total * factor + jnp.sum(probs, axis=2)
        accumulated = accumulated * factor[..., None] + jnp.einsum(
            "hqk,khd->hqd",
            probs.astype(jnp.bfloat16),
            value_rows,
            preferred_element_type=jnp.float32,
        )
        return (new_max, row_total, accumulated)

    carried = (
        jnp.full((hq, level), -1e30, jnp.float32),
        jnp.zeros((hq, level), jnp.float32),
        jnp.zeros((hq, level, HD), jnp.float32),
    )
    relay = [(i, i + 1) for i in range(nz - 1)]
    carried = attend(carried, pair, 0)
    block = lax.ppermute(pair, "z", relay)
    for distance in range(2, span + 1):
        block, carried = lax.optimization_barrier((block, carried))
        arriving = lax.ppermute(block, "z", relay)
        carried = attend(carried, block, distance - 1)
        block = arriving
    carried = attend(carried, block, span)
    run_max, row_total, accumulated = carried
    attended = (accumulated / row_total[..., None]).astype(jnp.bfloat16)
    attended = attended.transpose(1, 0, 2).reshape(level, hq * HD)

    c = lax.axis_index("c")
    swap = [(0, 1), (1, 0)]
    own_attended = lax.all_gather(attended, "y", axis=1, tiled=True)
    other_attended = lax.ppermute(own_attended, "c", swap)
    weight_cols, own_attended, other_attended = lax.optimization_barrier(
        (weight_cols, own_attended, other_attended)
    )
    chunk = out_weight.shape[1]
    weight_cols = weight_cols.reshape(weight_cols.shape[0], nz // 2, 2, chunk)
    own_weight = lax.dynamic_index_in_dim(weight_cols, c, axis=2, keepdims=False)
    other_weight = lax.ppermute(
        lax.dynamic_index_in_dim(weight_cols, 1 - c, axis=2, keepdims=False), "c", swap
    )
    own_weight = own_weight.reshape(own_weight.shape[0], -1)
    other_weight = other_weight.reshape(other_weight.shape[0], -1)
    partial_value = jnp.dot(own_attended, own_weight, preferred_element_type=jnp.float32)
    partial_value = partial_value + jnp.dot(
        other_attended, other_weight, preferred_element_type=jnp.float32
    )
    nx = lax.axis_size("x")
    pieces = partial_value.astype(jnp.bfloat16).reshape(NY, rows, nx * 2, chunk)
    pieces = pieces.transpose(0, 2, 1, 3).reshape(NY * nx * 2, rows, chunk)
    pieces = lax.all_to_all(pieces, ("y", "x", "c"), 0, 0, tiled=True)
    summed = pieces.reshape(NY, nx, 2, rows, chunk).astype(jnp.float32).sum(axis=1)
    hidden_states = summed.astype(jnp.bfloat16).transpose(2, 1, 0, 3).reshape(rows, 2 * NY * chunk)

    head_major = keys_values.reshape(rows, 2, heads, HD).transpose(1, 2, 0, 3)
    return (hidden_states, head_major)


def solution(mesh):
    seq, tensor = mesh.shape["seq"], mesh.shape["tensor"]
    assert seq % NY == 0 and tensor % 2 == 0
    grid = Mesh(
        mesh.devices.reshape(seq // NY, NY, tensor // 2, 2), ("z", "y", "x", "c")
    )
    s, t = ("z", "y"), ("x", "c")
    return jax.shard_map(
        local,
        mesh=grid,
        in_specs=(P(s, t), P(s, None, t), P(s), P(t, s)),
        out_specs=(P(s, t), P(None, t, s, None)),
        check_vma=False,
    )
```

```python
import math

import jax
import jax.numpy as jnp
from jax import lax
from jax.sharding import Mesh
from jax.sharding import PartitionSpec as P

HD = 128
NY = 4


def local(queries, keys_values, segment_ids, out_weight):
    rows = queries.shape[0]
    heads = queries.shape[1] // HD
    nz = lax.axis_size("z")
    z = lax.axis_index("z")
    level = NY * rows
    span = min(4, nz - 1)
    score_scale = 1.0 / math.sqrt(HD)
    half = out_weight.shape[1] // 2
    weight_cols = jnp.concatenate(
        [
            lax.all_gather(out_weight[:, :half], "z", axis=1, tiled=True).reshape(-1, nz, half),
            lax.all_gather(out_weight[:, half:], "z", axis=1, tiled=True).reshape(-1, nz, half),
        ],
        axis=2,
    ).reshape(out_weight.shape[0], nz * 2 * half)

    hq = heads // NY
    packed = jnp.concatenate(
        [queries.reshape(rows, 1, heads, HD), keys_values.reshape(rows, 2, heads, HD)], axis=1
    ).reshape(rows, 3, NY, hq, HD)
    seg_row = jnp.zeros((3 * hq * HD,), jnp.bfloat16).at[:rows].set(segment_ids.astype(jnp.bfloat16))
    seg_row = jnp.broadcast_to(seg_row.reshape(1, 3, 1, hq, HD), (1, 3, NY, hq, HD))
    packed = jnp.concatenate([packed, seg_row], axis=0)
    packed = lax.all_to_all(packed, "y", 2, 0, tiled=True).reshape(NY, rows + 1, 3, hq, HD)
    query_rows = packed[:, :rows, 0].reshape(level, hq, HD)
    pair = packed[:, :rows, 1:].reshape(level, 2, hq, HD)
    query_seg = packed[:, rows].reshape(NY, 3 * hq * HD)[:, :rows].reshape(level)

    extra = -(-level // (2 * hq * HD))
    seg_rows = jnp.zeros((extra * 2 * hq * HD,), jnp.bfloat16).at[:level].set(query_seg)
    pair = jnp.concatenate([pair, seg_rows.reshape(extra, 2, hq, HD)], axis=0)
    query_seg = query_seg.astype(jnp.int32)
    offsets = jnp.arange(level, dtype=jnp.int32)

    def attend(carried, block, distance):
        run_max, row_total, accumulated = carried
        source = z - distance
        key_seg = block[level:].reshape(-1)[:level].astype(jnp.int32)
        key_rows = block[:level, 0]
        value_rows = block[:level, 1]
        scores = (
            jnp.einsum("qhd,khd->hqk", query_rows, key_rows, preferred_element_type=jnp.float32)
            * score_scale
        )
        allowed = key_seg[None, :] == query_seg[:, None]
        if distance == 0:
            allowed = allowed & (offsets[None, :] <= offsets[:, None])
        else:
            allowed = allowed & (source >= 0)
        masked = jnp.where(allowed[None], scores, -1e30)
        new_max = jnp.maximum(run_max, jnp.max(masked, axis=2))
        probs = jnp.where(allowed[None], jnp.exp(masked - new_max[..., None]), 0.0)
        factor = jnp.exp(run_max - new_max)
        row_total = row_total * factor + jnp.sum(probs, axis=2)
        accumulated = accumulated * factor[..., None] + jnp.einsum(
            "hqk,khd->hqd",
            probs.astype(jnp.bfloat16),
            value_rows,
            preferred_element_type=jnp.float32,
        )
        return (new_max, row_total, accumulated)

    carried = (
        jnp.full((hq, level), -1e30, jnp.float32),
        jnp.zeros((hq, level), jnp.float32),
        jnp.zeros((hq, level, HD), jnp.float32),
    )
    relay = [(i, i + 1) for i in range(nz - 1)]
    carried = attend(carried, pair, 0)
    block = lax.ppermute(pair, "z", relay)
    for distance in range(2, span + 1):
        block, carried = lax.optimization_barrier((block, carried))
        arriving = lax.ppermute(block, "z", relay)
        carried = attend(carried, block, distance - 1)
        block = arriving
    carried = attend(carried, block, span)
    run_max, row_total, accumulated = carried
    attended = (accumulated / row_total[..., None]).astype(jnp.bfloat16)
    attended = attended.transpose(1, 0, 2).reshape(level, hq * HD)

    c = lax.axis_index("c")
    swap = [(0, 1), (1, 0)]
    own_attended = lax.all_gather(attended, "y", axis=1, tiled=True)
    other_attended = lax.ppermute(own_attended, "c", swap)
    weight_cols, own_attended, other_attended = lax.optimization_barrier(
        (weight_cols, own_attended, other_attended)
    )
    chunk = out_weight.shape[1]
    weight_cols = weight_cols.reshape(weight_cols.shape[0], nz // 2, 2, chunk)
    own_weight = lax.dynamic_index_in_dim(weight_cols, c, axis=2, keepdims=False)
    other_weight = lax.ppermute(
        lax.dynamic_index_in_dim(weight_cols, 1 - c, axis=2, keepdims=False), "c", swap
    )
    own_weight = own_weight.reshape(own_weight.shape[0], -1)
    other_weight = other_weight.reshape(other_weight.shape[0], -1)
    partial_value = jnp.dot(own_attended, own_weight, preferred_element_type=jnp.float32)
    partial_value = partial_value + jnp.dot(
        other_attended, other_weight, preferred_element_type=jnp.float32
    )
    nx = lax.axis_size("x")
    pieces = partial_value.astype(jnp.bfloat16).reshape(NY, rows, nx * 2, chunk)
    pieces = pieces.transpose(0, 2, 1, 3).reshape(NY * nx * 2, rows, chunk)
    pieces = lax.all_to_all(pieces, ("y", "x", "c"), 0, 0, tiled=True)
    summed = pieces.reshape(NY, nx, 2, rows, chunk).astype(jnp.float32).sum(axis=1)
    hidden_states = summed.astype(jnp.bfloat16).transpose(2, 1, 0, 3).reshape(rows, 2 * NY * chunk)

    head_major = keys_values.reshape(rows, 2, heads, HD).transpose(1, 2, 0, 3)
    return (hidden_states, head_major)


def solution(mesh):
    seq, tensor = mesh.shape["seq"], mesh.shape["tensor"]
    assert seq % NY == 0 and tensor % 2 == 0
    grid = Mesh(
        mesh.devices.reshape(seq // NY, NY, tensor // 2, 2), ("z", "y", "x", "c")
    )
    s, t = ("z", "y"), ("x", "c")
    return jax.shard_map(
        local,
        mesh=grid,
        in_specs=(P(s, t), P(s, None, t), P(s), P(t, s)),
        out_specs=(P(s, t), P(None, t, s, None)),
        check_vma=False,
    )
```

```python
import math

import jax
import jax.numpy as jnp
from jax import lax
from jax.sharding import Mesh
from jax.sharding import PartitionSpec as P

HD = 128
NY = 4


def local(queries, keys_values, segment_ids, out_weight):
    rows = queries.shape[0]
    heads = queries.shape[1] // HD
    nz = lax.axis_size("z")
    z = lax.axis_index("z")
    level = NY * rows
    span = min(4, nz - 1)
    score_scale = 1.0 / math.sqrt(HD)
    c = lax.axis_index("c")
    swap = [(0, 1), (1, 0)]
    half = out_weight.shape[1] // 2
    slab = jnp.concatenate([out_weight, lax.ppermute(out_weight, "c", swap)], axis=0)
    slab = lax.dynamic_slice_in_dim(slab, c * half, half, axis=1).T
    weight_rows = lax.all_gather(slab, "z", axis=0, tiled=True)

    hq = heads // NY
    packed = jnp.concatenate(
        [queries.reshape(rows, 1, heads, HD), keys_values.reshape(rows, 2, heads, HD)], axis=1
    ).reshape(rows, 3, NY, hq, HD)
    seg_row = jnp.zeros((3 * hq * HD,), jnp.bfloat16).at[:rows].set(segment_ids.astype(jnp.bfloat16))
    seg_row = jnp.broadcast_to(seg_row.reshape(1, 3, 1, hq, HD), (1, 3, NY, hq, HD))
    packed = jnp.concatenate([packed, seg_row], axis=0)
    packed = lax.all_to_all(packed, "y", 2, 0, tiled=True).reshape(NY, rows + 1, 3, hq, HD)
    query_rows = packed[:, :rows, 0].reshape(level, hq, HD)
    pair = packed[:, :rows, 1:].reshape(level, 2, hq, HD)
    query_seg = packed[:, rows].reshape(NY, 3 * hq * HD)[:, :rows].reshape(level)

    extra = -(-level // (2 * hq * HD))
    seg_rows = jnp.zeros((extra * 2 * hq * HD,), jnp.bfloat16).at[:level].set(query_seg)
    pair = jnp.concatenate([pair, seg_rows.reshape(extra, 2, hq, HD)], axis=0)
    query_seg = query_seg.astype(jnp.int32)
    offsets = jnp.arange(level, dtype=jnp.int32)

    def attend(carried, block, distance):
        run_max, row_total, accumulated = carried
        source = z - distance
        key_seg = block[level:].reshape(-1)[:level].astype(jnp.int32)
        key_rows = block[:level, 0]
        value_rows = block[:level, 1]
        scores = (
            jnp.einsum("qhd,khd->hqk", query_rows, key_rows, preferred_element_type=jnp.float32)
            * score_scale
        )
        allowed = key_seg[None, :] == query_seg[:, None]
        if distance == 0:
            allowed = allowed & (offsets[None, :] <= offsets[:, None])
        else:
            allowed = allowed & (source >= 0)
        masked = jnp.where(allowed[None], scores, -1e30)
        new_max = jnp.maximum(run_max, jnp.max(masked, axis=2))
        probs = jnp.where(allowed[None], jnp.exp(masked - new_max[..., None]), 0.0)
        factor = jnp.exp(run_max - new_max)
        row_total = row_total * factor + jnp.sum(probs, axis=2)
        accumulated = accumulated * factor[..., None] + jnp.einsum(
            "hqk,khd->hqd",
            probs.astype(jnp.bfloat16),
            value_rows,
            preferred_element_type=jnp.float32,
        )
        return (new_max, row_total, accumulated)

    carried = (
        jnp.full((hq, level), -1e30, jnp.float32),
        jnp.zeros((hq, level), jnp.float32),
        jnp.zeros((hq, level, HD), jnp.float32),
    )
    relay = [(i, i + 1) for i in range(nz - 1)]
    carried = attend(carried, pair, 0)
    block = lax.ppermute(pair, "z", relay)
    for distance in range(2, span + 1):
        block, carried = lax.optimization_barrier((block, carried))
        arriving = lax.ppermute(block, "z", relay)
        carried = attend(carried, block, distance - 1)
        block = arriving
    carried = attend(carried, block, span)
    run_max, row_total, accumulated = carried
    attended = (accumulated / row_total[..., None]).astype(jnp.bfloat16)
    attended = attended.transpose(1, 0, 2).reshape(level, hq * HD)

    own_attended = lax.all_gather(attended, "y", axis=1, tiled=True)
    other_attended = lax.ppermute(own_attended, "c", swap)
    weight_rows, own_attended, other_attended = lax.optimization_barrier(
        (weight_rows, own_attended, other_attended)
    )
    features = own_attended.shape[1]
    partial_value = jnp.einsum(
        "rk,nk->rn", own_attended, weight_rows[:, :features], preferred_element_type=jnp.float32
    ) + jnp.einsum(
        "rk,nk->rn", other_attended, weight_rows[:, features:], preferred_element_type=jnp.float32
    )
    nx = lax.axis_size("x")
    pieces = partial_value.astype(jnp.bfloat16).reshape(NY, rows, nx * 2, 2 * half)
    pieces = pieces.transpose(0, 2, 1, 3).reshape(NY * nx * 2, rows, 2 * half)
    pieces = lax.all_to_all(pieces, ("y", "x", "c"), 0, 0, tiled=True)
    summed = pieces.reshape(NY, nx, 2, rows, 2, half).astype(jnp.float32).sum(axis=1)
    hidden_states = summed.astype(jnp.bfloat16).transpose(2, 3, 0, 1, 4).reshape(rows, 4 * NY * half)

    head_major = keys_values.reshape(rows, 2, heads, HD).transpose(1, 2, 0, 3)
    return (hidden_states, head_major)


def solution(mesh):
    seq, tensor = mesh.shape["seq"], mesh.shape["tensor"]
    assert seq % NY == 0 and tensor % 2 == 0
    grid = Mesh(
        mesh.devices.reshape(seq // NY, NY, tensor // 2, 2), ("z", "y", "x", "c")
    )
    s, t = ("z", "y"), ("x", "c")
    return jax.shard_map(
        local,
        mesh=grid,
        in_specs=(P(s, t), P(s, None, t), P(s), P(t, s)),
        out_specs=(P(s, t), P(None, t, s, None)),
        check_vma=False,
    )
```

```python
import math

import jax
import jax.numpy as jnp
from jax import lax
from jax.sharding import Mesh
from jax.sharding import PartitionSpec as P

HD = 128
NY = 4


def local(queries, keys_values, segment_ids, out_weight):
    rows = queries.shape[0]
    heads = queries.shape[1] // HD
    nz = lax.axis_size("z")
    z = lax.axis_index("z")
    level = NY * rows
    span = min(4, nz - 1)
    score_scale = 1.0 / math.sqrt(HD)
    c = lax.axis_index("c")
    swap = [(0, 1), (1, 0)]
    half = out_weight.shape[1] // 2
    slab = jnp.concatenate([out_weight, lax.ppermute(out_weight, "c", swap)], axis=0)
    slab = lax.dynamic_slice_in_dim(slab, c * half, half, axis=1).T

    hq = heads // NY
    packed = jnp.concatenate(
        [queries.reshape(rows, 1, heads, HD), keys_values.reshape(rows, 2, heads, HD)], axis=1
    ).reshape(rows, 3, NY, hq, HD)
    seg_row = jnp.zeros((3 * hq * HD,), jnp.bfloat16).at[:rows].set(segment_ids.astype(jnp.bfloat16))
    seg_row = jnp.broadcast_to(seg_row.reshape(1, 3, 1, hq, HD), (1, 3, NY, hq, HD))
    packed = jnp.concatenate([packed, seg_row], axis=0)
    packed, slab = lax.optimization_barrier((packed, slab))
    weight_rows = lax.all_gather(slab, "z", axis=0, tiled=True)
    packed = lax.all_to_all(packed, "y", 2, 0, tiled=True).reshape(NY, rows + 1, 3, hq, HD)
    query_rows = packed[:, :rows, 0].reshape(level, hq, HD)
    pair = packed[:, :rows, 1:].reshape(level, 2, hq, HD)
    query_seg = packed[:, rows].reshape(NY, 3 * hq * HD)[:, :rows].reshape(level)

    extra = -(-level // (2 * hq * HD))
    seg_rows = jnp.zeros((extra * 2 * hq * HD,), jnp.bfloat16).at[:level].set(query_seg)
    pair = jnp.concatenate([pair, seg_rows.reshape(extra, 2, hq, HD)], axis=0)
    query_seg = query_seg.astype(jnp.int32)
    offsets = jnp.arange(level, dtype=jnp.int32)

    def attend(carried, block, distance):
        run_max, row_total, accumulated = carried
        source = z - distance
        key_seg = block[level:].reshape(-1)[:level].astype(jnp.int32)
        key_rows = block[:level, 0]
        value_rows = block[:level, 1]
        scores = (
            jnp.einsum("qhd,khd->hqk", query_rows, key_rows, preferred_element_type=jnp.float32)
            * score_scale
        )
        allowed = key_seg[None, :] == query_seg[:, None]
        if distance == 0:
            allowed = allowed & (offsets[None, :] <= offsets[:, None])
        else:
            allowed = allowed & (source >= 0)
        masked = jnp.where(allowed[None], scores, -1e30)
        new_max = jnp.maximum(run_max, jnp.max(masked, axis=2))
        probs = jnp.where(allowed[None], jnp.exp(masked - new_max[..., None]), 0.0)
        factor = jnp.exp(run_max - new_max)
        row_total = row_total * factor + jnp.sum(probs, axis=2)
        accumulated = accumulated * factor[..., None] + jnp.einsum(
            "hqk,khd->hqd",
            probs.astype(jnp.bfloat16),
            value_rows,
            preferred_element_type=jnp.float32,
        )
        return (new_max, row_total, accumulated)

    carried = (
        jnp.full((hq, level), -1e30, jnp.float32),
        jnp.zeros((hq, level), jnp.float32),
        jnp.zeros((hq, level, HD), jnp.float32),
    )
    relay = [(i, i + 1) for i in range(nz - 1)]
    carried = attend(carried, pair, 0)
    block = lax.ppermute(pair, "z", relay)
    for distance in range(2, span + 1):
        block, carried = lax.optimization_barrier((block, carried))
        arriving = lax.ppermute(block, "z", relay)
        carried = attend(carried, block, distance - 1)
        block = arriving
    carried = attend(carried, block, span)
    run_max, row_total, accumulated = carried
    attended = (accumulated / row_total[..., None]).astype(jnp.bfloat16)
    attended = attended.transpose(1, 0, 2).reshape(level, hq * HD)

    own_attended = lax.all_gather(attended, "y", axis=1, tiled=True)
    other_attended = lax.ppermute(own_attended, "c", swap)
    weight_rows, own_attended, other_attended = lax.optimization_barrier(
        (weight_rows, own_attended, other_attended)
    )
    features = own_attended.shape[1]
    partial_value = jnp.einsum(
        "rk,nk->rn", own_attended, weight_rows[:, :features], preferred_element_type=jnp.float32
    ) + jnp.einsum(
        "rk,nk->rn", other_attended, weight_rows[:, features:], preferred_element_type=jnp.float32
    )
    nx = lax.axis_size("x")
    pieces = partial_value.astype(jnp.bfloat16).reshape(NY, rows, nx * 2, 2 * half)
    pieces = pieces.transpose(0, 2, 1, 3).reshape(NY * nx * 2, rows, 2 * half)
    pieces = lax.all_to_all(pieces, ("y", "x", "c"), 0, 0, tiled=True)
    summed = pieces.reshape(NY, nx, 2, rows, 2, half).astype(jnp.float32).sum(axis=1)
    hidden_states = summed.astype(jnp.bfloat16).transpose(2, 3, 0, 1, 4).reshape(rows, 4 * NY * half)

    head_major = keys_values.reshape(rows, 2, heads, HD).transpose(1, 2, 0, 3)
    return (hidden_states, head_major)


def solution(mesh):
    seq, tensor = mesh.shape["seq"], mesh.shape["tensor"]
    assert seq % NY == 0 and tensor % 2 == 0
    grid = Mesh(
        mesh.devices.reshape(seq // NY, NY, tensor // 2, 2), ("z", "y", "x", "c")
    )
    s, t = ("z", "y"), ("x", "c")
    return jax.shard_map(
        local,
        mesh=grid,
        in_specs=(P(s, t), P(s, None, t), P(s), P(t, s)),
        out_specs=(P(s, t), P(None, t, s, None)),
        check_vma=False,
    )
```

```python
import math

import jax
import jax.numpy as jnp
from jax import lax
from jax.sharding import Mesh
from jax.sharding import PartitionSpec as P

HD = 128
NY = 4
MOST = 2161


def local(queries, keys_values, segment_ids, out_weight):
    rows = queries.shape[0]
    heads = queries.shape[1] // HD
    nz = lax.axis_size("z")
    z = lax.axis_index("z")
    level = NY * rows
    span = min(4, nz - 1)
    score_scale = 1.0 / math.sqrt(HD)
    c = lax.axis_index("c")
    swap = [(0, 1), (1, 0)]
    half = out_weight.shape[1] // 2
    slab = jnp.concatenate([out_weight, lax.ppermute(out_weight, "c", swap)], axis=0)
    slab = lax.dynamic_slice_in_dim(slab, c * half, half, axis=1).T
    weight_rows = lax.all_gather(slab, "z", axis=0, tiled=True)

    hq = heads // NY
    packed = jnp.concatenate(
        [queries.reshape(rows, 1, heads, HD), keys_values.reshape(rows, 2, heads, HD)], axis=1
    ).reshape(rows, 3, NY, hq, HD)
    seg_row = jnp.zeros((3 * hq * HD,), jnp.bfloat16).at[:rows].set(segment_ids.astype(jnp.bfloat16))
    seg_row = jnp.broadcast_to(seg_row.reshape(1, 3, 1, hq, HD), (1, 3, NY, hq, HD))
    packed = jnp.concatenate([packed, seg_row], axis=0)
    packed = lax.all_to_all(packed, "y", 2, 0, tiled=True).reshape(NY, rows + 1, 3, hq, HD)
    query_rows = packed[:, :rows, 0].reshape(level, hq, HD)
    pair = packed[:, :rows, 1:].reshape(level, 2, hq, HD)
    query_seg = packed[:, rows].reshape(NY, 3 * hq * HD)[:, :rows].reshape(level)

    extra = -(-level // (2 * hq * HD))
    seg_rows = jnp.zeros((extra * 2 * hq * HD,), jnp.bfloat16).at[:level].set(query_seg)
    pair = jnp.concatenate([pair, seg_rows.reshape(extra, 2, hq, HD)], axis=0)
    query_seg = query_seg.astype(jnp.int32)
    offsets = jnp.arange(level, dtype=jnp.int32)

    def attend(carried, block, distance):
        run_max, row_total, accumulated = carried
        source = z - distance
        keys = block.shape[0] - extra
        skipped = level - keys
        key_seg = block[keys:].reshape(-1)[skipped:level].astype(jnp.int32)
        key_rows = block[:keys, 0]
        value_rows = block[:keys, 1]
        scores = (
            jnp.einsum("qhd,khd->hqk", query_rows, key_rows, preferred_element_type=jnp.float32)
            * score_scale
        )
        allowed = key_seg[None, :] == query_seg[:, None]
        if distance == 0:
            allowed = allowed & (offsets[None, :] <= offsets[:, None])
        else:
            allowed = allowed & (source >= 0)
        masked = jnp.where(allowed[None], scores, -1e30)
        new_max = jnp.maximum(run_max, jnp.max(masked, axis=2))
        probs = jnp.where(allowed[None], jnp.exp(masked - new_max[..., None]), 0.0)
        factor = jnp.exp(run_max - new_max)
        row_total = row_total * factor + jnp.sum(probs, axis=2)
        accumulated = accumulated * factor[..., None] + jnp.einsum(
            "hqk,khd->hqd",
            probs.astype(jnp.bfloat16),
            value_rows,
            preferred_element_type=jnp.float32,
        )
        return (new_max, row_total, accumulated)

    carried = (
        jnp.full((hq, level), -1e30, jnp.float32),
        jnp.zeros((hq, level), jnp.float32),
        jnp.zeros((hq, level, HD), jnp.float32),
    )
    relay = [(i, i + 1) for i in range(nz - 1)]
    carried = attend(carried, pair, 0)
    block = lax.ppermute(pair, "z", relay)
    skip = min(max(0, span * level - (MOST - 1)), level) // 16 * 16
    for distance in range(2, span + 1):
        block, carried = lax.optimization_barrier((block, carried))
        outgoing = block
        if distance == span:
            outgoing = jnp.concatenate([block[skip:level], block[level:]], axis=0)
        arriving = lax.ppermute(outgoing, "z", relay)
        carried = attend(carried, block, distance - 1)
        block = arriving
    carried = attend(carried, block, span)
    run_max, row_total, accumulated = carried
    attended = (accumulated / row_total[..., None]).astype(jnp.bfloat16)
    attended = attended.transpose(1, 0, 2).reshape(level, hq * HD)

    own_attended = lax.all_gather(attended, "y", axis=1, tiled=True)
    other_attended = lax.ppermute(own_attended, "c", swap)
    weight_rows, own_attended, other_attended = lax.optimization_barrier(
        (weight_rows, own_attended, other_attended)
    )
    features = own_attended.shape[1]
    partial_value = jnp.einsum(
        "rk,nk->rn", own_attended, weight_rows[:, :features], preferred_element_type=jnp.float32
    ) + jnp.einsum(
        "rk,nk->rn", other_attended, weight_rows[:, features:], preferred_element_type=jnp.float32
    )
    nx = lax.axis_size("x")
    pieces = partial_value.astype(jnp.bfloat16).reshape(NY, rows, nx * 2, 2 * half)
    pieces = pieces.transpose(0, 2, 1, 3).reshape(NY * nx * 2, rows, 2 * half)
    pieces = lax.all_to_all(pieces, ("y", "x", "c"), 0, 0, tiled=True)
    summed = pieces.reshape(NY, nx, 2, rows, 2, half).astype(jnp.float32).sum(axis=1)
    hidden_states = summed.astype(jnp.bfloat16).transpose(2, 3, 0, 1, 4).reshape(rows, 4 * NY * half)

    head_major = keys_values.reshape(rows, 2, heads, HD).transpose(1, 2, 0, 3)
    return (hidden_states, head_major)


def solution(mesh):
    seq, tensor = mesh.shape["seq"], mesh.shape["tensor"]
    assert seq % NY == 0 and tensor % 2 == 0
    grid = Mesh(
        mesh.devices.reshape(seq // NY, NY, tensor // 2, 2), ("z", "y", "x", "c")
    )
    s, t = ("z", "y"), ("x", "c")
    return jax.shard_map(
        local,
        mesh=grid,
        in_specs=(P(s, t), P(s, None, t), P(s), P(t, s)),
        out_specs=(P(s, t), P(None, t, s, None)),
        check_vma=False,
    )
```

```python
import math

import jax
import jax.numpy as jnp
from jax import lax
from jax.sharding import Mesh
from jax.sharding import PartitionSpec as P

HD = 128
NY = 4


def local(queries, keys_values, segment_ids, out_weight):
    rows = queries.shape[0]
    heads = queries.shape[1] // HD
    nz = lax.axis_size("z")
    z = lax.axis_index("z")
    level = NY * rows
    span = min(4, nz - 1)
    score_scale = 1.0 / math.sqrt(HD)
    c = lax.axis_index("c")
    swap = [(0, 1), (1, 0)]
    half = out_weight.shape[1] // 2
    slab = jnp.concatenate([out_weight, lax.ppermute(out_weight, "c", swap)], axis=0)
    slab = lax.dynamic_slice_in_dim(slab, c * half, half, axis=1).T
    weight_rows = lax.all_gather(slab, "z", axis=0, tiled=True)

    hq = heads // NY
    packed = jnp.concatenate(
        [queries.reshape(rows, 1, heads, HD), keys_values.reshape(rows, 2, heads, HD)], axis=1
    ).reshape(rows, 3, NY, hq, HD)
    seg_row = jnp.zeros((3 * hq * HD,), jnp.bfloat16).at[:rows].set(segment_ids.astype(jnp.bfloat16))
    seg_row = jnp.broadcast_to(seg_row.reshape(1, 3, 1, hq, HD), (1, 3, NY, hq, HD))
    packed = jnp.concatenate([packed, seg_row], axis=0)
    packed = lax.all_to_all(packed, "y", 2, 0, tiled=True).reshape(NY, rows + 1, 3, hq, HD)
    query_rows = packed[:, :rows, 0].reshape(level, hq, HD)
    pair = packed[:, :rows, 1:].reshape(level, 2, hq, HD)
    query_seg = packed[:, rows].reshape(NY, 3 * hq * HD)[:, :rows].reshape(level)

    extra = -(-level // (2 * hq * HD))
    seg_rows = jnp.zeros((extra * 2 * hq * HD,), jnp.bfloat16).at[:level].set(query_seg)
    pair = jnp.concatenate([pair, seg_rows.reshape(extra, 2, hq, HD)], axis=0)
    query_seg = query_seg.astype(jnp.int32)
    offsets = jnp.arange(level, dtype=jnp.int32)

    def attend(carried, block, distance):
        run_max, row_total, accumulated = carried
        source = z - distance
        key_seg = block[level:].reshape(-1)[:level].astype(jnp.int32)
        key_rows = block[:level, 0]
        value_rows = block[:level, 1]
        scores = (
            jnp.einsum("qhd,khd->hqk", query_rows, key_rows, preferred_element_type=jnp.float32)
            * score_scale
        )
        allowed = key_seg[None, :] == query_seg[:, None]
        if distance == 0:
            allowed = allowed & (offsets[None, :] <= offsets[:, None])
        else:
            allowed = allowed & (source >= 0)
        masked = jnp.where(allowed[None], scores, -1e30)
        new_max = jnp.maximum(run_max, jnp.max(masked, axis=2))
        probs = jnp.where(allowed[None], jnp.exp(masked - new_max[..., None]), 0.0)
        factor = jnp.exp(run_max - new_max)
        row_total = row_total * factor + jnp.sum(probs, axis=2)
        accumulated = accumulated * factor[..., None] + jnp.einsum(
            "hqk,khd->hqd",
            probs.astype(jnp.bfloat16),
            value_rows,
            preferred_element_type=jnp.float32,
        )
        return (new_max, row_total, accumulated)

    carried = (
        jnp.full((hq, level), -1e30, jnp.float32),
        jnp.zeros((hq, level), jnp.float32),
        jnp.zeros((hq, level, HD), jnp.float32),
    )
    relay = [(i, i + 1) for i in range(nz - 1)]
    carried = attend(carried, pair, 0)
    block = lax.ppermute(pair, "z", relay)
    for distance in range(2, span + 1):
        block, carried = lax.optimization_barrier((block, carried))
        arriving = lax.ppermute(block, "z", relay)
        carried = attend(carried, block, distance - 1)
        block = arriving
    carried = attend(carried, block, span)
    run_max, row_total, accumulated = carried
    attended = (accumulated / row_total[..., None]).astype(jnp.bfloat16)
    attended = attended.transpose(1, 0, 2).reshape(level, hq * HD)

    own_attended = lax.all_gather(attended, "y", axis=1, tiled=True)
    other_attended = lax.ppermute(own_attended, "c", swap)
    chip_attended = jnp.concatenate([own_attended, other_attended], axis=1)
    weight_rows, chip_attended = lax.optimization_barrier((weight_rows, chip_attended))
    partial_value = jnp.einsum(
        "rk,nk->rn", chip_attended, weight_rows, preferred_element_type=jnp.float32
    )
    nx = lax.axis_size("x")
    pieces = partial_value.astype(jnp.bfloat16).reshape(NY, rows, nx * 2, 2 * half)
    pieces = pieces.transpose(0, 2, 1, 3).reshape(NY * nx * 2, rows, 2 * half)
    pieces = lax.all_to_all(pieces, ("y", "x", "c"), 0, 0, tiled=True)
    summed = pieces.reshape(NY, nx, 2, rows, 2, half).astype(jnp.float32).sum(axis=1)
    hidden_states = summed.astype(jnp.bfloat16).transpose(2, 3, 0, 1, 4).reshape(rows, 4 * NY * half)

    head_major = keys_values.reshape(rows, 2, heads, HD).transpose(1, 2, 0, 3)
    return (hidden_states, head_major)


def solution(mesh):
    seq, tensor = mesh.shape["seq"], mesh.shape["tensor"]
    assert seq % NY == 0 and tensor % 2 == 0
    grid = Mesh(
        mesh.devices.reshape(seq // NY, NY, tensor // 2, 2), ("z", "y", "x", "c")
    )
    s, t = ("z", "y"), ("x", "c")
    return jax.shard_map(
        local,
        mesh=grid,
        in_specs=(P(s, t), P(s, None, t), P(s), P(t, s)),
        out_specs=(P(s, t), P(None, t, s, None)),
        check_vma=False,
    )
```
